128 devices in a mesh: scene: 64 (over z, y, x), veh: 2 (over core).
Axes of the slice: x: 4, y: 4, z: 4, core: 2. Of those that a mesh axis runs over, the one named last changes fastest.
Arguments:
- features: bfloat16 [64, 4, 256, 16, 128], P('scene', 'veh'), may hold values from -64 to 64
- counts: int32 [64], P('scene'), may hold values from 2 to 4, as said below
- ego_ids: int32 [64], P('scene'), may hold values from 0 to 3, as said below
- req_tiles: int32 [64, 4, 2], P('scene', 'veh'), may hold values from 0 to 3, as said below
- req_count: int32 [64, 4], P('scene', 'veh'), may hold values from 1 to 2, as said below
- ego_embed: bfloat16 [256], replicated, may hold values from -8 to 8
- enc_weight: bfloat16 [9, 256, 256], replicated, may hold values from -0.125 to 0.125
- post_weight: bfloat16 [9, 256, 256], replicated, may hold values from -0.125 to 0.125
- cotangent: bfloat16 [64, 256, 16, 128], P('scene', None, 'veh'), may hold values from -6 to 6
Outputs:
- refined: bfloat16 [64, 256, 16, 128], P('scene', None, 'veh')
- feature_grad: float32 [64, 4, 256, 16, 128], P('scene', 'veh')
- enc_grad: float32 [9, 256, 256], replicated
- post_grad: float32 [9, 256, 256], replicated
- embed_grad: float32 [256], replicated
The draws below stay inside these ranges and needn't reach their ends.
Inputs may be any that keep to these rules, and one draw needn't show every extreme that they name: `counts`: some scene has all 4 vehicles. `ego_ids`: the ego is one of the scene's present vehicles; in some scene with all 4 vehicles in which the ego asks 2 tiles of every other vehicle, the ego is the last vehicle. `req_tiles`: the 2 tile ids of one vehicle are distinct. `req_count`: the ego's own entry and those of vehicles at or beyond the count are not used; in some scene with all 4 vehicles the ego asks 2 tiles of every other vehicle.
All inputs are finite; a program needn't handle non-finite values.
Results may differ from the reference program's by a relative error of at most 0.012.
The reference program's roundings to bfloat16 on the way count: a program that leaves them out, or rounds other values in their place, can miss the bound.
Values may be sent and summed in bfloat16 or wider, within the bound.
No kernel may reach another device: no remote copies, remote signals or barrier semaphores. Data moves between devices by JAX's collectives and lax.ppermute only.
A program may use at most 192 MiB of HBM per device.

```python
import jax
import jax.numpy as jnp
from jax import lax

C = 256
TILE = 32
ROWS = 16
TCOLS = 4
KMAX = 2
VEH = 4
SCENES = 64


def draw_ints(key):
    count_key, full_key, ego_key, asked_key, score_key = jax.random.split(jax.random.fold_in(key, 5), 5)
    lowest = max(2, VEH - 3)
    scene_ids = jnp.arange(SCENES)
    full_scene = jax.random.randint(full_key, (), 0, SCENES)
    counts = jax.random.randint(count_key, (SCENES,), lowest, VEH + 1)
    counts = jnp.where(scene_ids == full_scene, VEH, counts).astype(jnp.int32)
    ego_ids = jax.random.randint(ego_key, (SCENES,), 0, 1 << 20) % counts
    ego_ids = jnp.where(scene_ids == full_scene, VEH - 1, ego_ids).astype(jnp.int32)
    asked_count = jax.random.randint(asked_key, (SCENES, VEH), 1, KMAX + 1)
    asked_count = jnp.where(scene_ids[:, None] == full_scene, KMAX, asked_count).astype(jnp.int32)
    scores = jax.random.randint(score_key, (SCENES, VEH, TCOLS), 0, 1 << 16) * TCOLS + jnp.arange(TCOLS)
    picked = jnp.argsort(scores, axis=-1)[..., :KMAX].astype(jnp.int32)
    return (counts, ego_ids, picked, asked_count)


def draw_counts(key, part):
    return draw_ints(key)[0]


def draw_ego_ids(key, part):
    return draw_ints(key)[1]


def draw_req_tiles(key, part):
    return draw_ints(key)[2]


def draw_req_count(key, part):
    return draw_ints(key)[3]


def draw_features(key, part):
    base_key = jax.random.fold_in(jax.random.fold_in(key, 11), 0)
    full_shape = (SCENES, VEH, C, ROWS, TILE * TCOLS)
    values = jnp.clip(jax.random.normal(base_key, full_shape, jnp.float32), -6.0, 6.0)
    return values.astype(jnp.bfloat16)


def block_scale(stream_key, dims, cuts, low, top_value):
    def one(position, shards_of):
        heights = jax.random.uniform(jax.random.fold_in(jax.random.fold_in(stream_key, 6), position), (shards_of,), jnp.float32, low / len(cuts), top_value / len(cuts))
        return jnp.repeat(jnp.exp(heights), dims[position] // shards_of).reshape((-1,) + (1,) * (len(dims) - position - 1))

    loudness = one(*cuts[0])
    for cut in cuts[1:]:
        loudness = loudness * one(*cut)
    return loudness


def centred(key, shape, spread, bound, shards=(), dtype=jnp.bfloat16):
    gain = block_scale(key, shape, shards, -0.22, 0.18) if shards else 1.0
    array = jax.random.normal(key, shape, jnp.float32) * spread * gain
    return jnp.minimum(jnp.maximum(array, -bound), bound).astype(dtype)


def setup_inputs(seed: int = 0) -> dict:
    seeds = jax.random.split(jax.random.key(seed), 10)
    features = draw_features(jax.random.fold_in(seeds[9], 71), 0)
    counts = draw_counts(jax.random.fold_in(seeds[9], 71), 0)
    ego_ids = draw_ego_ids(jax.random.fold_in(seeds[9], 71), 0)
    req_tiles = draw_req_tiles(jax.random.fold_in(seeds[9], 71), 0)
    req_count = draw_req_count(jax.random.fold_in(seeds[9], 71), 0)
    ego_embed = centred(seeds[5], (C,), 2.0, 8.0)
    enc_weight = centred(seeds[6], (9, C, C), (9 * C) ** -0.5, 0.125)
    post_weight = centred(seeds[7], (9, C, C), (9 * C) ** -0.5, 0.125)
    cotangent = centred(seeds[8], (SCENES, C, ROWS, TILE * TCOLS), 1.0, 6.0, ((0, 64), (2, 2)))
    return {"features": features, "counts": counts, "ego_ids": ego_ids, "req_tiles": req_tiles, "req_count": req_count, "ego_embed": ego_embed, "enc_weight": enc_weight, "post_weight": post_weight, "cotangent": cotangent}


def pad_rows(source):
    return jnp.pad(source, [(0, 0)] * (source.ndim - 2) + [(2, 2), (0, 0)])


def tap_stack(padded, out_rows):
    breadth = padded.shape[-1]
    widened = jnp.pad(padded, [(0, 0)] * (padded.ndim - 1) + [(2, 2)])
    pieces = []
    for row_tap in range(3):
        for col_tap in range(3):
            pieces.append(widened[..., 2 * row_tap:2 * row_tap + out_rows, 2 * col_tap:2 * col_tap + breadth])
    return jnp.stack(pieces, axis=-4)


def conv_apply(weight, stacked):
    return jnp.einsum("tio,...tirw->...orw", weight.astype(jnp.float32), stacked.astype(jnp.float32), precision=lax.Precision.HIGHEST)


def conv_back(weight, stacked):
    return jnp.einsum("tio,...torw->...irw", weight[::-1].astype(jnp.float32), stacked.astype(jnp.float32), precision=lax.Precision.HIGHEST)


def silu_slope(values):
    sigma = jax.nn.sigmoid(values)
    return sigma * (1.0 + values * (1.0 - sigma))


def join_agents(query, partners, col_mask, ego_embed):
    query_wide = query.astype(jnp.float32)
    parts_wide = partners.astype(jnp.float32)
    channel_count = query.shape[-3]
    key_self = query_wide + ego_embed.astype(jnp.float32)[:, None, None]
    score_self = jnp.sum(query_wide * key_self, axis=-3) / channel_count
    score_part = jnp.sum(query_wide[..., None, :, :, :] * parts_wide, axis=-3) / channel_count
    live_cells = col_mask[..., :, None, :] > 0.5
    row_max = jnp.maximum(score_self, jnp.max(jnp.where(live_cells, score_part, -jnp.inf), axis=-3))
    self_exp = jnp.exp(score_self - row_max)
    part_exp = jnp.where(live_cells, jnp.exp(jnp.minimum(score_part - row_max[..., None, :, :], 0.0)), 0.0)
    denominator = self_exp + jnp.sum(part_exp, axis=-3)
    self_weight = self_exp / denominator
    part_weight = part_exp / denominator[..., None, :, :]
    joined_map = self_weight[..., None, :, :] * query_wide + jnp.sum(part_weight[..., :, None, :, :] * parts_wide, axis=-4)
    return joined_map, self_weight, part_weight


def attend_back(query, partners, ego_embed, self_weight, part_weight, joined_grad):
    query_wide = query.astype(jnp.float32)
    parts_wide = partners.astype(jnp.float32)
    channel_count = query.shape[-3]
    self_dot = jnp.sum(joined_grad * query_wide, axis=-3)
    part_dot = jnp.sum(joined_grad[..., None, :, :, :] * parts_wide, axis=-3)
    mean_dot = self_weight * self_dot + jnp.sum(part_weight * part_dot, axis=-3)
    slope_self = self_weight * (self_dot - mean_dot)
    slope_part = part_weight * (part_dot - mean_dot[..., None, :, :])
    twice_key = 2.0 * query_wide + ego_embed.astype(jnp.float32)[:, None, None]
    ego_term = self_weight[..., None, :, :] * joined_grad + (slope_self[..., None, :, :] * twice_key + jnp.sum(slope_part[..., :, None, :, :] * parts_wide, axis=-4)) / channel_count
    part_grads = part_weight[..., :, None, :, :] * joined_grad[..., None, :, :, :] + slope_part[..., :, None, :, :] * query_wide[..., None, :, :, :] / channel_count
    embed_terms = jnp.sum(slope_self[..., None, :, :] * query_wide, axis=(-2, -1)) / channel_count
    embed_partial = jnp.sum(embed_terms.reshape(-1, channel_count), axis=0)
    return ego_term.astype(jnp.bfloat16), part_grads.astype(jnp.bfloat16), embed_partial


def scene_step(feature_maps, count, ego_id, tiles_asked, asked_count, cot_map, ego_embed, enc_weight, post_weight):
    vehicles, channel_count, height, breadth = feature_maps.shape
    tile_count = breadth // TILE
    veh_ids = jnp.arange(vehicles)
    live_count = jnp.where((veh_ids < count) & (veh_ids != ego_id), asked_count, 0)
    onehot = ((tiles_asked[:, :, None] == jnp.arange(tile_count)[None, None, :]) & (jnp.arange(KMAX)[None, :, None] < live_count[:, None, None])).astype(jnp.float32)
    col_mask = jnp.repeat(jnp.sum(onehot, axis=1), TILE, axis=-1)
    enc_stack = tap_stack(pad_rows(feature_maps), height)
    enc_pre = conv_apply(enc_weight, enc_stack)
    encoded = (feature_maps.astype(jnp.float32) + jax.nn.silu(enc_pre)).astype(jnp.bfloat16)
    ego_map = encoded[ego_id]
    partners = (encoded.astype(jnp.float32) * col_mask[:, None, None, :]).astype(jnp.bfloat16)
    joined_map, self_weight, part_weight = join_agents(ego_map, partners, col_mask, ego_embed)
    joined_bf = joined_map.astype(jnp.bfloat16)
    post_stack = tap_stack(pad_rows(joined_bf), height)
    post_pre = conv_apply(post_weight, post_stack)
    refined = (joined_bf.astype(jnp.float32) + jax.nn.silu(post_pre)).astype(jnp.bfloat16)
    grad_map = cot_map.astype(jnp.float32)
    post_slope = (grad_map * silu_slope(post_pre)).astype(jnp.bfloat16)
    post_partial = jnp.einsum("tirw,orw->tio", post_stack.astype(jnp.float32), post_slope.astype(jnp.float32), precision=lax.Precision.HIGHEST)
    joined_grad = grad_map + conv_back(post_weight, tap_stack(pad_rows(post_slope), height))
    ego_term, part_grads, embed_partial = attend_back(ego_map, partners, ego_embed, self_weight, part_weight, joined_grad)
    is_ego = (veh_ids == ego_id).astype(jnp.float32)[:, None, None, None]
    encoded_grad = part_grads.astype(jnp.float32) + is_ego * ego_term.astype(jnp.float32)[None]
    enc_slope = (encoded_grad * silu_slope(enc_pre)).astype(jnp.bfloat16)
    enc_partial = jnp.einsum("vtirw,vorw->tio", enc_stack.astype(jnp.float32), enc_slope.astype(jnp.float32), precision=lax.Precision.HIGHEST)
    feature_grad = encoded_grad + conv_back(enc_weight, tap_stack(pad_rows(enc_slope), height))
    return refined, feature_grad, enc_partial, post_partial, embed_partial


def reference(features, counts, ego_ids, req_tiles, req_count, ego_embed, enc_weight, post_weight, cotangent):
    def one_scene(inputs):
        feature_maps, count, ego_id, tiles_asked, asked_count, cot_map = inputs
        return scene_step(feature_maps, count, ego_id, tiles_asked, asked_count, cot_map, ego_embed, enc_weight, post_weight)

    refined, feature_grad, enc_parts, post_parts, embed_parts = lax.map(one_scene, (features, counts, ego_ids, req_tiles, req_count, cotangent))
    return refined, feature_grad, jnp.sum(enc_parts, axis=0), jnp.sum(post_parts, axis=0), jnp.sum(embed_parts, axis=0)
```

```python
import jax
import jax.numpy as jnp
from jax import lax
from jax.sharding import PartitionSpec as P

TILE = 32
KMAX = 2


def pad_rows(source):
    return jnp.pad(source, [(0, 0)] * (source.ndim - 2) + [(2, 2), (0, 0)])


def tap_stack(padded, out_rows):
    breadth = padded.shape[-1]
    widened = jnp.pad(padded, [(0, 0)] * (padded.ndim - 1) + [(2, 2)])
    pieces = []
    for row_tap in range(3):
        for col_tap in range(3):
            pieces.append(
                widened[
                    ..., 2 * row_tap : 2 * row_tap + out_rows, 2 * col_tap : 2 * col_tap + breadth
                ]
            )
    return jnp.stack(pieces, axis=-4)


def conv_apply(weight, stacked):
    return jnp.einsum("tio,btirw->borw", weight, stacked, preferred_element_type=jnp.float32)


def conv_back(weight, stacked):
    return jnp.einsum("tio,btorw->birw", weight[::-1], stacked, preferred_element_type=jnp.float32)


def weight_partial(stacked, slope):
    return jnp.einsum("btirw,borw->tio", stacked, slope, preferred_element_type=jnp.float32)


def silu_slope(values):
    sigma = jax.nn.sigmoid(values)
    return sigma * (1.0 + values * (1.0 - sigma))


def join_agents(query, partners, col_mask, ego_embed):
    query_wide = query.astype(jnp.float32)
    parts_wide = partners.astype(jnp.float32)
    channel_count = query.shape[-3]
    key_self = query_wide + ego_embed.astype(jnp.float32)[:, None, None]
    score_self = jnp.sum(query_wide * key_self, axis=-3) / channel_count
    score_part = jnp.sum(query_wide[..., None, :, :, :] * parts_wide, axis=-3) / channel_count
    live_cells = col_mask[..., :, None, :] > 0.5
    row_max = jnp.maximum(score_self, jnp.max(jnp.where(live_cells, score_part, -jnp.inf), axis=-3))
    self_exp = jnp.exp(score_self - row_max)
    part_exp = jnp.where(
        live_cells, jnp.exp(jnp.minimum(score_part - row_max[..., None, :, :], 0.0)), 0.0
    )
    denominator = self_exp + jnp.sum(part_exp, axis=-3)
    self_weight = self_exp / denominator
    part_weight = part_exp / denominator[..., None, :, :]
    joined_map = self_weight[..., None, :, :] * query_wide + jnp.sum(
        part_weight[..., :, None, :, :] * parts_wide, axis=-4
    )
    return (joined_map, self_weight, part_weight)


def attend_back(query, partners, ego_embed, self_weight, part_weight, joined_grad):
    query_wide = query.astype(jnp.float32)
    parts_wide = partners.astype(jnp.float32)
    channel_count = query.shape[-3]
    self_dot = jnp.sum(joined_grad * query_wide, axis=-3)
    part_dot = jnp.sum(joined_grad[..., None, :, :, :] * parts_wide, axis=-3)
    mean_dot = self_weight * self_dot + jnp.sum(part_weight * part_dot, axis=-3)
    slope_self = self_weight * (self_dot - mean_dot)
    slope_part = part_weight * (part_dot - mean_dot[..., None, :, :])
    twice_key = 2.0 * query_wide + ego_embed.astype(jnp.float32)[:, None, None]
    ego_term = (
        self_weight[..., None, :, :] * joined_grad
        + (
            slope_self[..., None, :, :] * twice_key
            + jnp.sum(slope_part[..., :, None, :, :] * parts_wide, axis=-4)
        )
        / channel_count
    )
    part_grads = (
        part_weight[..., :, None, :, :] * joined_grad[..., None, :, :, :]
        + slope_part[..., :, None, :, :] * query_wide[..., None, :, :, :] / channel_count
    )
    embed_terms = jnp.sum(slope_self[..., None, :, :] * query_wide, axis=(-2, -1)) / channel_count
    embed_partial = jnp.sum(embed_terms, axis=0)
    return (ego_term.astype(jnp.bfloat16), part_grads.astype(jnp.bfloat16), embed_partial)


def body(
    features, counts, ego_ids, req_tiles, req_count, ego_embed, enc_weight, post_weight, cotangent
):
    batch_size, local_veh, channels, height, breadth = features.shape
    tile_count = breadth // TILE
    devices_veh = lax.axis_size("veh")
    vehicles = local_veh * devices_veh
    veh_here = lax.axis_index("veh") * local_veh + jnp.arange(local_veh)
    ego_local = ego_ids[:, None] == veh_here[None, :]
    ego_mask = ego_local.astype(jnp.float32)
    ego_device = jnp.sum(ego_mask, axis=1)[:, None, None, None]
    present = (veh_here[None, :] < counts[:, None]) & jnp.logical_not(ego_local)
    live_count = jnp.where(present, req_count, 0)
    slot_ids = jnp.arange(KMAX)
    tile_ids = jnp.arange(tile_count)
    own_onehot = (
        (req_tiles[:, :, :, None] == tile_ids[None, None, None, :])
        & (slot_ids[None, None, :, None] < live_count[:, :, None, None])
    ).astype(jnp.bfloat16)
    flat_maps = features.reshape(batch_size * local_veh, channels, height, breadth)
    enc_stack = tap_stack(pad_rows(flat_maps), height)
    enc_pre = conv_apply(enc_weight, enc_stack)
    encoded_flat = (flat_maps.astype(jnp.float32) + jax.nn.silu(enc_pre)).astype(jnp.bfloat16)
    encoded = encoded_flat.reshape(batch_size, local_veh, channels, height, breadth)
    query = jnp.einsum(
        "bv,bvchw->bchw", ego_mask.astype(jnp.bfloat16), encoded, preferred_element_type=jnp.float32
    ).astype(jnp.bfloat16)
    tiled_map = encoded.reshape(batch_size, local_veh, channels, height, tile_count, TILE)
    send_slots = jnp.einsum(
        "bvkt,bvchtw->bvkchw", own_onehot, tiled_map, preferred_element_type=jnp.float32
    ).astype(jnp.bfloat16)
    send_flat = send_slots.reshape(batch_size, local_veh, KMAX, channels, height * TILE)
    gathered, onehots = (
        lax.all_gather(send_flat, "veh", axis=1, tiled=True),
        lax.all_gather(own_onehot, "veh", axis=1, tiled=True),
    )
    gathered = gathered.reshape(batch_size, vehicles, KMAX, channels, height, TILE)
    partners = jnp.einsum(
        "bskt,bskchw->bschtw", onehots, gathered, preferred_element_type=jnp.float32
    ).astype(jnp.bfloat16)
    partners = partners.reshape(batch_size, vehicles, channels, height, breadth)
    col_mask = jnp.repeat(jnp.sum(onehots.astype(jnp.float32), axis=2), TILE, axis=-1)
    grad_full = (
        lax.all_gather(cotangent, "veh", axis=2, tiled=True).astype(jnp.float32) * ego_device
    )
    joined_map, self_weight, part_weight = join_agents(query, partners, col_mask, ego_embed)
    joined_bf = joined_map.astype(jnp.bfloat16)
    post_stack = tap_stack(pad_rows(joined_bf), height)
    post_pre = conv_apply(post_weight, post_stack)
    refined_full = joined_bf.astype(jnp.float32) + jax.nn.silu(post_pre)
    refined_full = refined_full.astype(jnp.bfloat16).astype(jnp.float32) * ego_device
    refined = lax.psum_scatter(
        refined_full.astype(jnp.bfloat16), "veh", scatter_dimension=2, tiled=True
    )
    post_slope = (grad_full * silu_slope(post_pre)).astype(jnp.bfloat16)
    post_partial = weight_partial(post_stack, post_slope)
    weight_size = post_partial.size
    joined_grad = grad_full + conv_back(post_weight, tap_stack(pad_rows(post_slope), height))
    ego_term, part_grads, embed_partial = attend_back(
        query, partners, ego_embed, self_weight, part_weight, joined_grad
    )
    post_flat = jnp.concatenate([post_partial.reshape(-1), embed_partial])
    post_sum = lax.psum(post_flat, ("scene", "veh"))
    post_grad = post_sum[:weight_size].reshape(post_partial.shape)
    embed_grad = post_sum[weight_size:]
    part_tiles = part_grads.reshape(batch_size, vehicles, channels, height, tile_count, TILE)
    slot_grads = jnp.einsum(
        "bskt,bschtw->bskchw", onehots, part_tiles, preferred_element_type=jnp.float32
    )
    slot_grads = (
        slot_grads.reshape(batch_size, vehicles, KMAX, channels, height * TILE)
        * ego_device[:, :, :, :, None]
    )
    slot_bf = slot_grads.astype(jnp.bfloat16)
    low_half = slot_bf[:, :local_veh]
    high_half = slot_bf[:, local_veh:]
    on_low = lax.axis_index("veh") == 0
    outgoing = jnp.where(on_low, high_half, low_half)
    kept = jnp.where(on_low, low_half, high_half)
    incoming = lax.ppermute(outgoing, "veh", [(0, 1), (1, 0)])
    returned = (kept.astype(jnp.float32) + incoming.astype(jnp.float32)).astype(jnp.bfloat16)
    returned = returned.reshape(batch_size, local_veh, KMAX, channels, height, TILE)
    own_term = ego_mask[:, :, None, None, None] * ego_term.astype(jnp.float32)[:, None]
    placed = jnp.einsum(
        "bvkt,bvkchw->bvchtw", own_onehot, returned, preferred_element_type=jnp.float32
    )
    encoded_grad = own_term + placed.reshape(batch_size, local_veh, channels, height, breadth)
    encoded_grad = encoded_grad.reshape(batch_size * local_veh, channels, height, breadth)
    enc_slope = (encoded_grad * silu_slope(enc_pre)).astype(jnp.bfloat16)
    enc_partial = weight_partial(enc_stack, enc_slope)
    feature_grad = encoded_grad + conv_back(enc_weight, tap_stack(pad_rows(enc_slope), height))
    enc_partial, post_sum = lax.optimization_barrier((enc_partial, post_sum))
    enc_grad = lax.psum(enc_partial, ("scene", "veh"))
    return (
        refined,
        feature_grad.reshape(batch_size, local_veh, channels, height, breadth),
        enc_grad,
        post_grad,
        embed_grad,
    )


def solution(mesh):
    in_specs = (
        P("scene", "veh", None, None, None),
        P("scene"),
        P("scene"),
        P("scene", "veh", None),
        P("scene", "veh"),
        P(),
        P(),
        P(),
        P("scene", None, "veh", None),
    )
    out_specs = (P("scene", None, "veh", None), P("scene", "veh", None, None, None), P(), P(), P())
    return jax.shard_map(body, mesh=mesh, in_specs=in_specs, out_specs=out_specs, check_vma=False)
```

```python
import jax
import jax.numpy as jnp
from jax import lax
from jax.sharding import PartitionSpec as P

TILE = 32
KMAX = 2


def pad_rows(source):
    return jnp.pad(source, [(0, 0)] * (source.ndim - 2) + [(2, 2), (0, 0)])


def tap_stack(padded, out_rows):
    breadth = padded.shape[-1]
    widened = jnp.pad(padded, [(0, 0)] * (padded.ndim - 1) + [(2, 2)])
    pieces = []
    for row_tap in range(3):
        for col_tap in range(3):
            pieces.append(
                widened[
                    ..., 2 * row_tap : 2 * row_tap + out_rows, 2 * col_tap : 2 * col_tap + breadth
                ]
            )
    return jnp.stack(pieces, axis=-4)


def conv_apply(weight, stacked):
    return jnp.einsum("tio,btirw->borw", weight, stacked, preferred_element_type=jnp.float32)


def conv_back(weight, stacked):
    return jnp.einsum("tio,btorw->birw", weight[::-1], stacked, preferred_element_type=jnp.float32)


def weight_partial(stacked, slope):
    return jnp.einsum("btirw,borw->tio", stacked, slope, preferred_element_type=jnp.float32)


def silu_slope(values):
    sigma = jax.nn.sigmoid(values)
    return sigma * (1.0 + values * (1.0 - sigma))


def join_agents(query, partners, col_mask, ego_embed):
    query_wide = query.astype(jnp.float32)
    parts_wide = partners.astype(jnp.float32)
    channel_count = query.shape[-3]
    key_self = query_wide + ego_embed.astype(jnp.float32)[:, None, None]
    score_self = jnp.sum(query_wide * key_self, axis=-3) / channel_count
    score_part = jnp.sum(query_wide[..., None, :, :, :] * parts_wide, axis=-3) / channel_count
    live_cells = col_mask[..., :, None, :] > 0.5
    row_max = jnp.maximum(score_self, jnp.max(jnp.where(live_cells, score_part, -jnp.inf), axis=-3))
    self_exp = jnp.exp(score_self - row_max)
    part_exp = jnp.where(
        live_cells, jnp.exp(jnp.minimum(score_part - row_max[..., None, :, :], 0.0)), 0.0
    )
    denominator = self_exp + jnp.sum(part_exp, axis=-3)
    self_weight = self_exp / denominator
    part_weight = part_exp / denominator[..., None, :, :]
    joined_map = self_weight[..., None, :, :] * query_wide + jnp.sum(
        part_weight[..., :, None, :, :] * parts_wide, axis=-4
    )
    return (joined_map, self_weight, part_weight)


def attend_back(query, partners, ego_embed, self_weight, part_weight, joined_grad):
    query_wide = query.astype(jnp.float32)
    parts_wide = partners.astype(jnp.float32)
    channel_count = query.shape[-3]
    self_dot = jnp.sum(joined_grad * query_wide, axis=-3)
    part_dot = jnp.sum(joined_grad[..., None, :, :, :] * parts_wide, axis=-3)
    mean_dot = self_weight * self_dot + jnp.sum(part_weight * part_dot, axis=-3)
    slope_self = self_weight * (self_dot - mean_dot)
    slope_part = part_weight * (part_dot - mean_dot[..., None, :, :])
    twice_key = 2.0 * query_wide + ego_embed.astype(jnp.float32)[:, None, None]
    ego_term = (
        self_weight[..., None, :, :] * joined_grad
        + (
            slope_self[..., None, :, :] * twice_key
            + jnp.sum(slope_part[..., :, None, :, :] * parts_wide, axis=-4)
        )
        / channel_count
    )
    part_grads = (
        part_weight[..., :, None, :, :] * joined_grad[..., None, :, :, :]
        + slope_part[..., :, None, :, :] * query_wide[..., None, :, :, :] / channel_count
    )
    embed_terms = jnp.sum(slope_self[..., None, :, :] * query_wide, axis=(-2, -1)) / channel_count
    embed_partial = jnp.sum(embed_terms, axis=0)
    return (ego_term.astype(jnp.bfloat16), part_grads.astype(jnp.bfloat16), embed_partial)


def body(
    features, counts, ego_ids, req_tiles, req_count, ego_embed, enc_weight, post_weight, cotangent
):
    batch_size, local_veh, channels, height, breadth = features.shape
    tile_count = breadth // TILE
    devices_veh = lax.axis_size("veh")
    vehicles = local_veh * devices_veh
    veh_here = lax.axis_index("veh") * local_veh + jnp.arange(local_veh)
    ego_local = ego_ids[:, None] == veh_here[None, :]
    ego_mask = ego_local.astype(jnp.float32)
    ego_device = jnp.sum(ego_mask, axis=1)[:, None, None, None]
    present = (veh_here[None, :] < counts[:, None]) & jnp.logical_not(ego_local)
    live_count = jnp.where(present, req_count, 0)
    slot_ids = jnp.arange(KMAX)
    tile_ids = jnp.arange(tile_count)
    own_onehot = (
        (req_tiles[:, :, :, None] == tile_ids[None, None, None, :])
        & (slot_ids[None, None, :, None] < live_count[:, :, None, None])
    ).astype(jnp.bfloat16)
    flat_maps = features.reshape(batch_size * local_veh, channels, height, breadth)
    enc_stack = tap_stack(pad_rows(flat_maps), height)
    enc_pre = conv_apply(enc_weight, enc_stack)
    encoded_flat = (flat_maps.astype(jnp.float32) + jax.nn.silu(enc_pre)).astype(jnp.bfloat16)
    encoded = encoded_flat.reshape(batch_size, local_veh, channels, height, breadth)
    query = jnp.einsum(
        "bv,bvchw->bchw", ego_mask.astype(jnp.bfloat16), encoded, preferred_element_type=jnp.float32
    ).astype(jnp.bfloat16)
    tiled_map = encoded.reshape(batch_size, local_veh, channels, height, tile_count, TILE)
    send_slots = jnp.einsum(
        "bvkt,bvchtw->bvkchw", own_onehot, tiled_map, preferred_element_type=jnp.float32
    ).astype(jnp.bfloat16)
    send_flat = send_slots.reshape(batch_size, local_veh, KMAX, channels, height * TILE)
    gathered, onehots = (
        lax.all_gather(send_flat, "veh", axis=1, tiled=True),
        lax.all_gather(own_onehot, "veh", axis=1, tiled=True),
    )
    gathered = gathered.reshape(batch_size, vehicles, KMAX, channels, height, TILE)
    partners = jnp.einsum(
        "bskt,bskchw->bschtw", onehots, gathered, preferred_element_type=jnp.float32
    ).astype(jnp.bfloat16)
    partners = partners.reshape(batch_size, vehicles, channels, height, breadth)
    col_mask = jnp.repeat(jnp.sum(onehots.astype(jnp.float32), axis=2), TILE, axis=-1)
    grad_full = (
        lax.all_gather(cotangent, "veh", axis=2, tiled=True).astype(jnp.float32) * ego_device
    )
    joined_map, self_weight, part_weight = join_agents(query, partners, col_mask, ego_embed)
    joined_bf = joined_map.astype(jnp.bfloat16)
    post_stack = tap_stack(pad_rows(joined_bf), height)
    post_pre = conv_apply(post_weight, post_stack)
    refined_full = joined_bf.astype(jnp.float32) + jax.nn.silu(post_pre)
    refined_full = refined_full.astype(jnp.bfloat16).astype(jnp.float32) * ego_device
    refined = lax.psum_scatter(
        refined_full.astype(jnp.bfloat16), "veh", scatter_dimension=2, tiled=True
    )
    post_slope = (grad_full * silu_slope(post_pre)).astype(jnp.bfloat16)
    post_partial = weight_partial(post_stack, post_slope)
    joined_grad = grad_full + conv_back(post_weight, tap_stack(pad_rows(post_slope), height))
    ego_term, part_grads, embed_partial = attend_back(
        query, partners, ego_embed, self_weight, part_weight, joined_grad
    )
    part_tiles = part_grads.reshape(batch_size, vehicles, channels, height, tile_count, TILE)
    slot_grads = jnp.einsum(
        "bskt,bschtw->bskchw", onehots, part_tiles, preferred_element_type=jnp.float32
    )
    slot_grads = (
        slot_grads.reshape(batch_size, vehicles, KMAX, channels, height * TILE)
        * ego_device[:, :, :, :, None]
    )
    returned = lax.psum_scatter(
        slot_grads.astype(jnp.bfloat16), "veh", scatter_dimension=1, tiled=True
    )
    returned = returned.reshape(batch_size, local_veh, KMAX, channels, height, TILE)
    own_term = ego_mask[:, :, None, None, None] * ego_term.astype(jnp.float32)[:, None]
    placed = jnp.einsum(
        "bvkt,bvkchw->bvchtw", own_onehot, returned, preferred_element_type=jnp.float32
    )
    encoded_grad = own_term + placed.reshape(batch_size, local_veh, channels, height, breadth)
    encoded_grad = encoded_grad.reshape(batch_size * local_veh, channels, height, breadth)
    enc_slope = (encoded_grad * silu_slope(enc_pre)).astype(jnp.bfloat16)
    enc_partial = weight_partial(enc_stack, enc_slope)
    feature_grad = encoded_grad + conv_back(enc_weight, tap_stack(pad_rows(enc_slope), height))
    weight_size = enc_partial.size
    grad_flat = jnp.concatenate(
        [enc_partial.reshape(-1), post_partial.reshape(-1), embed_partial]
    )
    grad_sum = lax.psum(grad_flat, ("scene", "veh"))
    enc_grad = grad_sum[:weight_size].reshape(enc_partial.shape)
    post_grad = grad_sum[weight_size : 2 * weight_size].reshape(post_partial.shape)
    embed_grad = grad_sum[2 * weight_size :]
    return (
        refined,
        feature_grad.reshape(batch_size, local_veh, channels, height, breadth),
        enc_grad,
        post_grad,
        embed_grad,
    )


def solution(mesh):
    in_specs = (
        P("scene", "veh", None, None, None),
        P("scene"),
        P("scene"),
        P("scene", "veh", None),
        P("scene", "veh"),
        P(),
        P(),
        P(),
        P("scene", None, "veh", None),
    )
    out_specs = (P("scene", None, "veh", None), P("scene", "veh", None, None, None), P(), P(), P())
    return jax.shard_map(body, mesh=mesh, in_specs=in_specs, out_specs=out_specs, check_vma=False)
```

```python
import jax
import jax.numpy as jnp
from jax import lax
from jax.sharding import PartitionSpec as P

TILE = 32
KMAX = 2


def conv_apply(weight, maps):
    kernel = weight.reshape(3, 3, weight.shape[1], weight.shape[2])
    return lax.conv_general_dilated(
        maps,
        kernel,
        (1, 1),
        ((2, 2), (2, 2)),
        rhs_dilation=(2, 2),
        dimension_numbers=("NCHW", "HWIO", "NCHW"),
        preferred_element_type=jnp.float32,
    )


def conv_back(weight, slope):
    kernel = weight[::-1].reshape(3, 3, weight.shape[1], weight.shape[2])
    return lax.conv_general_dilated(
        slope,
        kernel,
        (1, 1),
        ((2, 2), (2, 2)),
        rhs_dilation=(2, 2),
        dimension_numbers=("NCHW", "HWOI", "NCHW"),
        preferred_element_type=jnp.float32,
    )


def weight_partial(maps, slope):
    taps = lax.conv_general_dilated(
        maps,
        slope,
        (2, 2),
        ((2, 2), (2, 2)),
        dimension_numbers=("CNHW", "IOHW", "HWNC"),
        preferred_element_type=jnp.float32,
    )
    return taps.reshape(9, maps.shape[1], slope.shape[1])


def silu_slope(values):
    sigma = jax.nn.sigmoid(values)
    return sigma * (1.0 + values * (1.0 - sigma))


def join_agents(query, partners, col_mask, ego_embed):
    query_wide = query.astype(jnp.float32)
    parts_wide = partners.astype(jnp.float32)
    channel_count = query.shape[-3]
    key_self = query_wide + ego_embed.astype(jnp.float32)[:, None, None]
    score_self = jnp.sum(query_wide * key_self, axis=-3) / channel_count
    score_part = jnp.sum(query_wide[..., None, :, :, :] * parts_wide, axis=-3) / channel_count
    live_cells = col_mask[..., :, None, :] > 0.5
    row_max = jnp.maximum(score_self, jnp.max(jnp.where(live_cells, score_part, -jnp.inf), axis=-3))
    self_exp = jnp.exp(score_self - row_max)
    part_exp = jnp.where(
        live_cells, jnp.exp(jnp.minimum(score_part - row_max[..., None, :, :], 0.0)), 0.0
    )
    denominator = self_exp + jnp.sum(part_exp, axis=-3)
    self_weight = self_exp / denominator
    part_weight = part_exp / denominator[..., None, :, :]
    joined_map = self_weight[..., None, :, :] * query_wide + jnp.sum(
        part_weight[..., :, None, :, :] * parts_wide, axis=-4
    )
    return (joined_map, self_weight, part_weight)


def attend_back(query, partners, ego_embed, self_weight, part_weight, joined_grad):
    query_wide = query.astype(jnp.float32)
    parts_wide = partners.astype(jnp.float32)
    channel_count = query.shape[-3]
    self_dot = jnp.sum(joined_grad * query_wide, axis=-3)
    part_dot = jnp.sum(joined_grad[..., None, :, :, :] * parts_wide, axis=-3)
    mean_dot = self_weight * self_dot + jnp.sum(part_weight * part_dot, axis=-3)
    slope_self = self_weight * (self_dot - mean_dot)
    slope_part = part_weight * (part_dot - mean_dot[..., None, :, :])
    twice_key = 2.0 * query_wide + ego_embed.astype(jnp.float32)[:, None, None]
    ego_term = (
        self_weight[..., None, :, :] * joined_grad
        + (
            slope_self[..., None, :, :] * twice_key
            + jnp.sum(slope_part[..., :, None, :, :] * parts_wide, axis=-4)
        )
        / channel_count
    )
    part_grads = (
        part_weight[..., :, None, :, :] * joined_grad[..., None, :, :, :]
        + slope_part[..., :, None, :, :] * query_wide[..., None, :, :, :] / channel_count
    )
    embed_terms = jnp.sum(slope_self[..., None, :, :] * query_wide, axis=(-2, -1)) / channel_count
    embed_partial = jnp.sum(embed_terms, axis=0)
    return (ego_term.astype(jnp.bfloat16), part_grads.astype(jnp.bfloat16), embed_partial)


def body(
    features, counts, ego_ids, req_tiles, req_count, ego_embed, enc_weight, post_weight, cotangent
):
    batch_size, local_veh, channels, height, breadth = features.shape
    tile_count = breadth // TILE
    devices_veh = lax.axis_size("veh")
    vehicles = local_veh * devices_veh
    veh_here = lax.axis_index("veh") * local_veh + jnp.arange(local_veh)
    ego_local = ego_ids[:, None] == veh_here[None, :]
    ego_mask = ego_local.astype(jnp.float32)
    ego_device = jnp.sum(ego_mask, axis=1)[:, None, None, None]
    present = (veh_here[None, :] < counts[:, None]) & jnp.logical_not(ego_local)
    live_count = jnp.where(present, req_count, 0)
    slot_ids = jnp.arange(KMAX)
    tile_ids = jnp.arange(tile_count)
    own_onehot = (
        (req_tiles[:, :, :, None] == tile_ids[None, None, None, :])
        & (slot_ids[None, None, :, None] < live_count[:, :, None, None])
    ).astype(jnp.bfloat16)
    flat_maps = features.reshape(batch_size * local_veh, channels, height, breadth)
    enc_pre = conv_apply(enc_weight, flat_maps)
    encoded_flat = (flat_maps.astype(jnp.float32) + jax.nn.silu(enc_pre)).astype(jnp.bfloat16)
    encoded = encoded_flat.reshape(batch_size, local_veh, channels, height, breadth)
    query = jnp.einsum(
        "bv,bvchw->bchw", ego_mask.astype(jnp.bfloat16), encoded, preferred_element_type=jnp.float32
    ).astype(jnp.bfloat16)
    tiled_map = encoded.reshape(batch_size, local_veh, channels, height, tile_count, TILE)
    send_slots = jnp.einsum(
        "bvkt,bvchtw->bvkchw", own_onehot, tiled_map, preferred_element_type=jnp.float32
    ).astype(jnp.bfloat16)
    send_flat = send_slots.reshape(batch_size, local_veh, KMAX, channels, height * TILE)
    gathered, onehots = (
        lax.all_gather(send_flat, "veh", axis=1, tiled=True),
        lax.all_gather(own_onehot, "veh", axis=1, tiled=True),
    )
    gathered = gathered.reshape(batch_size, vehicles, KMAX, channels, height, TILE)
    partners = jnp.einsum(
        "bskt,bskchw->bschtw", onehots, gathered, preferred_element_type=jnp.float32
    ).astype(jnp.bfloat16)
    partners = partners.reshape(batch_size, vehicles, channels, height, breadth)
    col_mask = jnp.repeat(jnp.sum(onehots.astype(jnp.float32), axis=2), TILE, axis=-1)
    grad_full = (
        lax.all_gather(cotangent, "veh", axis=2, tiled=True).astype(jnp.float32) * ego_device
    )
    joined_map, self_weight, part_weight = join_agents(query, partners, col_mask, ego_embed)
    joined_bf = joined_map.astype(jnp.bfloat16)
    post_pre = conv_apply(post_weight, joined_bf)
    refined_full = joined_bf.astype(jnp.float32) + jax.nn.silu(post_pre)
    refined_full = refined_full.astype(jnp.bfloat16).astype(jnp.float32) * ego_device
    refined = lax.psum_scatter(
        refined_full.astype(jnp.bfloat16), "veh", scatter_dimension=2, tiled=True
    )
    post_slope = (grad_full * silu_slope(post_pre)).astype(jnp.bfloat16)
    post_partial = weight_partial(joined_bf, post_slope)
    joined_grad = grad_full + conv_back(post_weight, post_slope)
    ego_term, part_grads, embed_partial = attend_back(
        query, partners, ego_embed, self_weight, part_weight, joined_grad
    )
    part_tiles = part_grads.reshape(batch_size, vehicles, channels, height, tile_count, TILE)
    slot_grads = jnp.einsum(
        "bskt,bschtw->bskchw", onehots, part_tiles, preferred_element_type=jnp.float32
    )
    slot_grads = (
        slot_grads.reshape(batch_size, vehicles, KMAX, channels, height * TILE)
        * ego_device[:, :, :, :, None]
    )
    returned = lax.psum_scatter(
        slot_grads.astype(jnp.bfloat16), "veh", scatter_dimension=1, tiled=True
    )
    returned = returned.reshape(batch_size, local_veh, KMAX, channels, height, TILE)
    own_term = ego_mask[:, :, None, None, None] * ego_term.astype(jnp.float32)[:, None]
    placed = jnp.einsum(
        "bvkt,bvkchw->bvchtw", own_onehot, returned, preferred_element_type=jnp.float32
    )
    encoded_grad = own_term + placed.reshape(batch_size, local_veh, channels, height, breadth)
    encoded_grad = encoded_grad.reshape(batch_size * local_veh, channels, height, breadth)
    enc_slope = (encoded_grad * silu_slope(enc_pre)).astype(jnp.bfloat16)
    enc_partial = weight_partial(flat_maps, enc_slope)
    feature_grad = encoded_grad + conv_back(enc_weight, enc_slope)
    weight_size = enc_partial.size
    grad_flat = jnp.concatenate(
        [enc_partial.reshape(-1), post_partial.reshape(-1), embed_partial]
    )
    grad_sum = lax.psum(grad_flat, ("scene", "veh"))
    enc_grad = grad_sum[:weight_size].reshape(enc_partial.shape)
    post_grad = grad_sum[weight_size : 2 * weight_size].reshape(post_partial.shape)
    embed_grad = grad_sum[2 * weight_size :]
    return (
        refined,
        feature_grad.reshape(batch_size, local_veh, channels, height, breadth),
        enc_grad,
        post_grad,
        embed_grad,
    )


def solution(mesh):
    in_specs = (
        P("scene", "veh", None, None, None),
        P("scene"),
        P("scene"),
        P("scene", "veh", None),
        P("scene", "veh"),
        P(),
        P(),
        P(),
        P("scene", None, "veh", None),
    )
    out_specs = (P("scene", None, "veh", None), P("scene", "veh", None, None, None), P(), P(), P())
    return jax.shard_map(body, mesh=mesh, in_specs=in_specs, out_specs=out_specs, check_vma=False)
```

```python
import jax
import jax.numpy as jnp
from jax import lax
from jax.sharding import PartitionSpec as P

TILE = 32
KMAX = 2
LANES = 128


def ring_shift(stride, size, shift, total):
    pairs = []
    for source in range(total):
        place = (source // stride) % size
        pairs.append((source, source + (((place + shift) % size) - place) * stride))
    return pairs


def torus_psum(flat, parts=3):
    total = lax.axis_size("scene")
    side = round(total ** (1.0 / 3.0))
    axes = [(side * side, side), (side, side), (1, side)]
    veh_count = lax.axis_size("veh")
    length = flat.shape[0]
    unit = parts * veh_count * total * LANES
    padded = jnp.pad(flat, (0, (-length) % unit)).reshape(parts, -1, LANES)
    veh_id = lax.axis_index("veh")
    scene_id = lax.axis_index("scene")
    swap = [(0, 1), (1, 0)]
    results = []
    for part in range(parts):
        halves = padded[part].reshape(veh_count, -1, LANES)
        on_low = veh_id == 0
        outgoing = jnp.where(on_low, halves[1], halves[0])
        current = jnp.where(on_low, halves[0], halves[1]) + lax.ppermute(outgoing, "veh", swap)
        order = [axes[(part + k) % 3] for k in range(3)]
        for stride, size in order:
            place = (scene_id // stride) % size
            chunks = current.reshape(size, -1, LANES)
            current = lax.dynamic_index_in_dim(chunks, place, 0, keepdims=False)
            for shift in range(1, size):
                piece = lax.dynamic_index_in_dim(chunks, (place + shift) % size, 0, keepdims=False)
                current = current + lax.ppermute(piece, "scene", ring_shift(stride, size, shift, total))
        for stride, size in reversed(order):
            place = (scene_id // stride) % size
            got = [current] + [
                lax.ppermute(current, "scene", ring_shift(stride, size, shift, total))
                for shift in range(1, size)
            ]
            backward = jnp.concatenate(got[::-1] + got[::-1], axis=0)
            start = ((size - (place + 1) % size) % size) * current.shape[0]
            current = lax.dynamic_slice_in_dim(backward, start, size * current.shape[0], 0)
        other = lax.ppermute(current, "veh", swap)
        results.append(jnp.where(veh_id == 0, jnp.concatenate([current, other]), jnp.concatenate([other, current])))
    return jnp.stack(results).reshape(-1)[:length]


def pad_rows(source):
    return jnp.pad(source, [(0, 0)] * (source.ndim - 2) + [(2, 2), (0, 0)])


def tap_stack(padded, out_rows):
    breadth = padded.shape[-1]
    widened = jnp.pad(padded, [(0, 0)] * (padded.ndim - 1) + [(2, 2)])
    pieces = []
    for row_tap in range(3):
        for col_tap in range(3):
            pieces.append(
                widened[
                    ..., 2 * row_tap : 2 * row_tap + out_rows, 2 * col_tap : 2 * col_tap + breadth
                ]
            )
    return jnp.stack(pieces, axis=-4)


def conv_apply(weight, stacked):
    return jnp.einsum("tio,btirw->borw", weight, stacked, preferred_element_type=jnp.float32)


def conv_back(weight, stacked):
    return jnp.einsum("tio,btorw->birw", weight[::-1], stacked, preferred_element_type=jnp.float32)


def weight_partial(stacked, slope):
    return jnp.einsum("btirw,borw->tio", stacked, slope, preferred_element_type=jnp.float32)


def silu_slope(values):
    sigma = jax.nn.sigmoid(values)
    return sigma * (1.0 + values * (1.0 - sigma))


def join_agents(query, partners, col_mask, ego_embed):
    query_wide = query.astype(jnp.float32)
    parts_wide = partners.astype(jnp.float32)
    channel_count = query.shape[-3]
    key_self = query_wide + ego_embed.astype(jnp.float32)[:, None, None]
    score_self = jnp.sum(query_wide * key_self, axis=-3) / channel_count
    score_part = jnp.sum(query_wide[..., None, :, :, :] * parts_wide, axis=-3) / channel_count
    live_cells = col_mask[..., :, None, :] > 0.5
    row_max = jnp.maximum(score_self, jnp.max(jnp.where(live_cells, score_part, -jnp.inf), axis=-3))
    self_exp = jnp.exp(score_self - row_max)
    part_exp = jnp.where(
        live_cells, jnp.exp(jnp.minimum(score_part - row_max[..., None, :, :], 0.0)), 0.0
    )
    denominator = self_exp + jnp.sum(part_exp, axis=-3)
    self_weight = self_exp / denominator
    part_weight = part_exp / denominator[..., None, :, :]
    joined_map = self_weight[..., None, :, :] * query_wide + jnp.sum(
        part_weight[..., :, None, :, :] * parts_wide, axis=-4
    )
    return (joined_map, self_weight, part_weight)


def attend_back(query, partners, ego_embed, self_weight, part_weight, joined_grad):
    query_wide = query.astype(jnp.float32)
    parts_wide = partners.astype(jnp.float32)
    channel_count = query.shape[-3]
    self_dot = jnp.sum(joined_grad * query_wide, axis=-3)
    part_dot = jnp.sum(joined_grad[..., None, :, :, :] * parts_wide, axis=-3)
    mean_dot = self_weight * self_dot + jnp.sum(part_weight * part_dot, axis=-3)
    slope_self = self_weight * (self_dot - mean_dot)
    slope_part = part_weight * (part_dot - mean_dot[..., None, :, :])
    twice_key = 2.0 * query_wide + ego_embed.astype(jnp.float32)[:, None, None]
    ego_term = (
        self_weight[..., None, :, :] * joined_grad
        + (
            slope_self[..., None, :, :] * twice_key
            + jnp.sum(slope_part[..., :, None, :, :] * parts_wide, axis=-4)
        )
        / channel_count
    )
    part_grads = (
        part_weight[..., :, None, :, :] * joined_grad[..., None, :, :, :]
        + slope_part[..., :, None, :, :] * query_wide[..., None, :, :, :] / channel_count
    )
    embed_terms = jnp.sum(slope_self[..., None, :, :] * query_wide, axis=(-2, -1)) / channel_count
    embed_partial = jnp.sum(embed_terms, axis=0)
    return (ego_term.astype(jnp.bfloat16), part_grads.astype(jnp.bfloat16), embed_partial)


def body(
    features, counts, ego_ids, req_tiles, req_count, ego_embed, enc_weight, post_weight, cotangent
):
    batch_size, local_veh, channels, height, breadth = features.shape
    tile_count = breadth // TILE
    devices_veh = lax.axis_size("veh")
    vehicles = local_veh * devices_veh
    veh_here = lax.axis_index("veh") * local_veh + jnp.arange(local_veh)
    ego_local = ego_ids[:, None] == veh_here[None, :]
    ego_mask = ego_local.astype(jnp.float32)
    ego_device = jnp.sum(ego_mask, axis=1)[:, None, None, None]
    present = (veh_here[None, :] < counts[:, None]) & jnp.logical_not(ego_local)
    live_count = jnp.where(present, req_count, 0)
    slot_ids = jnp.arange(KMAX)
    tile_ids = jnp.arange(tile_count)
    own_onehot = (
        (req_tiles[:, :, :, None] == tile_ids[None, None, None, :])
        & (slot_ids[None, None, :, None] < live_count[:, :, None, None])
    ).astype(jnp.bfloat16)
    flat_maps = features.reshape(batch_size * local_veh, channels, height, breadth)
    enc_stack = tap_stack(pad_rows(flat_maps), height)
    enc_pre = conv_apply(enc_weight, enc_stack)
    encoded_flat = (flat_maps.astype(jnp.float32) + jax.nn.silu(enc_pre)).astype(jnp.bfloat16)
    encoded = encoded_flat.reshape(batch_size, local_veh, channels, height, breadth)
    query = jnp.einsum(
        "bv,bvchw->bchw", ego_mask.astype(jnp.bfloat16), encoded, preferred_element_type=jnp.float32
    ).astype(jnp.bfloat16)
    tiled_map = encoded.reshape(batch_size, local_veh, channels, height, tile_count, TILE)
    send_slots = jnp.einsum(
        "bvkt,bvchtw->bvkchw", own_onehot, tiled_map, preferred_element_type=jnp.float32
    ).astype(jnp.bfloat16)
    send_flat = send_slots.reshape(batch_size, local_veh, KMAX, channels, height * TILE)
    gathered, onehots = (
        lax.all_gather(send_flat, "veh", axis=1, tiled=True),
        lax.all_gather(own_onehot, "veh", axis=1, tiled=True),
    )
    gathered = gathered.reshape(batch_size, vehicles, KMAX, channels, height, TILE)
    partners = jnp.einsum(
        "bskt,bskchw->bschtw", onehots, gathered, preferred_element_type=jnp.float32
    ).astype(jnp.bfloat16)
    partners = partners.reshape(batch_size, vehicles, channels, height, breadth)
    col_mask = jnp.repeat(jnp.sum(onehots.astype(jnp.float32), axis=2), TILE, axis=-1)
    grad_full = (
        lax.all_gather(cotangent, "veh", axis=2, tiled=True).astype(jnp.float32) * ego_device
    )
    joined_map, self_weight, part_weight = join_agents(query, partners, col_mask, ego_embed)
    joined_bf = joined_map.astype(jnp.bfloat16)
    post_stack = tap_stack(pad_rows(joined_bf), height)
    post_pre = conv_apply(post_weight, post_stack)
    refined_full = joined_bf.astype(jnp.float32) + jax.nn.silu(post_pre)
    refined_full = refined_full.astype(jnp.bfloat16).astype(jnp.float32) * ego_device
    refined = lax.psum_scatter(
        refined_full.astype(jnp.bfloat16), "veh", scatter_dimension=2, tiled=True
    )
    post_slope = (grad_full * silu_slope(post_pre)).astype(jnp.bfloat16)
    post_partial = weight_partial(post_stack, post_slope)
    weight_size = post_partial.size
    joined_grad = grad_full + conv_back(post_weight, tap_stack(pad_rows(post_slope), height))
    ego_term, part_grads, embed_partial = attend_back(
        query, partners, ego_embed, self_weight, part_weight, joined_grad
    )
    post_flat = jnp.concatenate([post_partial.reshape(-1), embed_partial])
    post_sum = lax.psum(post_flat, ("scene", "veh"))
    post_grad = post_sum[:weight_size].reshape(post_partial.shape)
    embed_grad = post_sum[weight_size:]
    part_tiles = part_grads.reshape(batch_size, vehicles, channels, height, tile_count, TILE)
    slot_grads = jnp.einsum(
        "bskt,bschtw->bskchw", onehots, part_tiles, preferred_element_type=jnp.float32
    )
    slot_grads = (
        slot_grads.reshape(batch_size, vehicles, KMAX, channels, height * TILE)
        * ego_device[:, :, :, :, None]
    )
    slot_bf = slot_grads.astype(jnp.bfloat16)
    low_half = slot_bf[:, :local_veh]
    high_half = slot_bf[:, local_veh:]
    on_low = lax.axis_index("veh") == 0
    outgoing = jnp.where(on_low, high_half, low_half)
    kept = jnp.where(on_low, low_half, high_half)
    incoming = lax.ppermute(outgoing, "veh", [(0, 1), (1, 0)])
    returned = (kept.astype(jnp.float32) + incoming.astype(jnp.float32)).astype(jnp.bfloat16)
    returned = returned.reshape(batch_size, local_veh, KMAX, channels, height, TILE)
    own_term = ego_mask[:, :, None, None, None] * ego_term.astype(jnp.float32)[:, None]
    placed = jnp.einsum(
        "bvkt,bvkchw->bvchtw", own_onehot, returned, preferred_element_type=jnp.float32
    )
    encoded_grad = own_term + placed.reshape(batch_size, local_veh, channels, height, breadth)
    encoded_grad = encoded_grad.reshape(batch_size * local_veh, channels, height, breadth)
    enc_slope = (encoded_grad * silu_slope(enc_pre)).astype(jnp.bfloat16)
    enc_partial = weight_partial(enc_stack, enc_slope)
    feature_grad = encoded_grad + conv_back(enc_weight, tap_stack(pad_rows(enc_slope), height))
    enc_grad = torus_psum(enc_partial.reshape(-1), parts=1).reshape(enc_partial.shape)
    return (
        refined,
        feature_grad.reshape(batch_size, local_veh, channels, height, breadth),
        enc_grad,
        post_grad,
        embed_grad,
    )


def solution(mesh):
    in_specs = (
        P("scene", "veh", None, None, None),
        P("scene"),
        P("scene"),
        P("scene", "veh", None),
        P("scene", "veh"),
        P(),
        P(),
        P(),
        P("scene", None, "veh", None),
    )
    out_specs = (P("scene", None, "veh", None), P("scene", "veh", None, None, None), P(), P(), P())
    return jax.shard_map(body, mesh=mesh, in_specs=in_specs, out_specs=out_specs, check_vma=False)
```

```python
import jax
import jax.numpy as jnp
from jax import lax
from jax.sharding import PartitionSpec as P

TILE = 32
KMAX = 2
LANES = 128


def ring_shift(stride, size, shift, total):
    pairs = []
    for source in range(total):
        place = (source // stride) % size
        pairs.append((source, source + (((place + shift) % size) - place) * stride))
    return pairs


def torus_psum(flat, parts=3):
    total = lax.axis_size("scene")
    side = round(total ** (1.0 / 3.0))
    axes = [(side * side, side), (side, side), (1, side)]
    veh_count = lax.axis_size("veh")
    length = flat.shape[0]
    unit = parts * veh_count * total * LANES
    padded = jnp.pad(flat, (0, (-length) % unit)).reshape(parts, -1, LANES)
    veh_id = lax.axis_index("veh")
    scene_id = lax.axis_index("scene")
    swap = [(0, 1), (1, 0)]
    results = []
    for part in range(parts):
        halves = padded[part].reshape(veh_count, -1, LANES)
        on_low = veh_id == 0
        outgoing = jnp.where(on_low, halves[1], halves[0])
        current = jnp.where(on_low, halves[0], halves[1]) + lax.ppermute(outgoing, "veh", swap)
        order = [axes[(part + k) % 3] for k in range(3)]
        for stride, size in order:
            place = (scene_id // stride) % size
            chunks = current.reshape(size, -1, LANES)
            current = lax.dynamic_index_in_dim(chunks, place, 0, keepdims=False)
            for shift in range(1, size):
                piece = lax.dynamic_index_in_dim(chunks, (place + shift) % size, 0, keepdims=False)
                current = current + lax.ppermute(piece, "scene", ring_shift(stride, size, shift, total))
        for stride, size in reversed(order):
            place = (scene_id // stride) % size
            got = [current] + [
                lax.ppermute(current, "scene", ring_shift(stride, size, shift, total))
                for shift in range(1, size)
            ]
            backward = jnp.concatenate(got[::-1] + got[::-1], axis=0)
            start = ((size - (place + 1) % size) % size) * current.shape[0]
            current = lax.dynamic_slice_in_dim(backward, start, size * current.shape[0], 0)
        other = lax.ppermute(current, "veh", swap)
        results.append(jnp.where(veh_id == 0, jnp.concatenate([current, other]), jnp.concatenate([other, current])))
    return jnp.stack(results).reshape(-1)[:length]


def pad_rows(source):
    return jnp.pad(source, [(0, 0)] * (source.ndim - 2) + [(2, 2), (0, 0)])


def tap_stack(padded, out_rows):
    breadth = padded.shape[-1]
    widened = jnp.pad(padded, [(0, 0)] * (padded.ndim - 1) + [(2, 2)])
    pieces = []
    for row_tap in range(3):
        for col_tap in range(3):
            pieces.append(
                widened[
                    ..., 2 * row_tap : 2 * row_tap + out_rows, 2 * col_tap : 2 * col_tap + breadth
                ]
            )
    return jnp.stack(pieces, axis=-4)


def conv_apply(weight, stacked):
    return jnp.einsum("tio,btirw->borw", weight, stacked, preferred_element_type=jnp.float32)


def conv_back(weight, stacked):
    return jnp.einsum("tio,btorw->birw", weight[::-1], stacked, preferred_element_type=jnp.float32)


def weight_partial(stacked, slope):
    return jnp.einsum("btirw,borw->tio", stacked, slope, preferred_element_type=jnp.float32)


def silu_slope(values):
    sigma = jax.nn.sigmoid(values)
    return sigma * (1.0 + values * (1.0 - sigma))


def join_agents(query, partners, col_mask, ego_embed):
    query_wide = query.astype(jnp.float32)
    parts_wide = partners.astype(jnp.float32)
    channel_count = query.shape[-3]
    key_self = query_wide + ego_embed.astype(jnp.float32)[:, None, None]
    score_self = jnp.sum(query_wide * key_self, axis=-3) / channel_count
    score_part = jnp.sum(query_wide[..., None, :, :, :] * parts_wide, axis=-3) / channel_count
    live_cells = col_mask[..., :, None, :] > 0.5
    row_max = jnp.maximum(score_self, jnp.max(jnp.where(live_cells, score_part, -jnp.inf), axis=-3))
    self_exp = jnp.exp(score_self - row_max)
    part_exp = jnp.where(
        live_cells, jnp.exp(jnp.minimum(score_part - row_max[..., None, :, :], 0.0)), 0.0
    )
    denominator = self_exp + jnp.sum(part_exp, axis=-3)
    self_weight = self_exp / denominator
    part_weight = part_exp / denominator[..., None, :, :]
    joined_map = self_weight[..., None, :, :] * query_wide + jnp.sum(
        part_weight[..., :, None, :, :] * parts_wide, axis=-4
    )
    return (joined_map, self_weight, part_weight)


def attend_back(query, partners, ego_embed, self_weight, part_weight, joined_grad):
    query_wide = query.astype(jnp.float32)
    parts_wide = partners.astype(jnp.float32)
    channel_count = query.shape[-3]
    self_dot = jnp.sum(joined_grad * query_wide, axis=-3)
    part_dot = jnp.sum(joined_grad[..., None, :, :, :] * parts_wide, axis=-3)
    mean_dot = self_weight * self_dot + jnp.sum(part_weight * part_dot, axis=-3)
    slope_self = self_weight * (self_dot - mean_dot)
    slope_part = part_weight * (part_dot - mean_dot[..., None, :, :])
    twice_key = 2.0 * query_wide + ego_embed.astype(jnp.float32)[:, None, None]
    ego_term = (
        self_weight[..., None, :, :] * joined_grad
        + (
            slope_self[..., None, :, :] * twice_key
            + jnp.sum(slope_part[..., :, None, :, :] * parts_wide, axis=-4)
        )
        / channel_count
    )
    part_grads = (
        part_weight[..., :, None, :, :] * joined_grad[..., None, :, :, :]
        + slope_part[..., :, None, :, :] * query_wide[..., None, :, :, :] / channel_count
    )
    embed_terms = jnp.sum(slope_self[..., None, :, :] * query_wide, axis=(-2, -1)) / channel_count
    embed_partial = jnp.sum(embed_terms, axis=0)
    return (ego_term.astype(jnp.bfloat16), part_grads.astype(jnp.bfloat16), embed_partial)


def body(
    features, counts, ego_ids, req_tiles, req_count, ego_embed, enc_weight, post_weight, cotangent
):
    batch_size, local_veh, channels, height, breadth = features.shape
    tile_count = breadth // TILE
    devices_veh = lax.axis_size("veh")
    vehicles = local_veh * devices_veh
    veh_here = lax.axis_index("veh") * local_veh + jnp.arange(local_veh)
    ego_local = ego_ids[:, None] == veh_here[None, :]
    ego_mask = ego_local.astype(jnp.float32)
    ego_device = jnp.sum(ego_mask, axis=1)[:, None, None, None]
    present = (veh_here[None, :] < counts[:, None]) & jnp.logical_not(ego_local)
    live_count = jnp.where(present, req_count, 0)
    slot_ids = jnp.arange(KMAX)
    tile_ids = jnp.arange(tile_count)
    own_onehot = (
        (req_tiles[:, :, :, None] == tile_ids[None, None, None, :])
        & (slot_ids[None, None, :, None] < live_count[:, :, None, None])
    ).astype(jnp.bfloat16)
    flat_maps = features.reshape(batch_size * local_veh, channels, height, breadth)
    enc_stack = tap_stack(pad_rows(flat_maps), height)
    enc_pre = conv_apply(enc_weight, enc_stack)
    encoded_flat = (flat_maps.astype(jnp.float32) + jax.nn.silu(enc_pre)).astype(jnp.bfloat16)
    encoded = encoded_flat.reshape(batch_size, local_veh, channels, height, breadth)
    query = jnp.einsum(
        "bv,bvchw->bchw", ego_mask.astype(jnp.bfloat16), encoded, preferred_element_type=jnp.float32
    ).astype(jnp.bfloat16)
    tiled_map = encoded.reshape(batch_size, local_veh, channels, height, tile_count, TILE)
    send_slots = jnp.einsum(
        "bvkt,bvchtw->bvkchw", own_onehot, tiled_map, preferred_element_type=jnp.float32
    ).astype(jnp.bfloat16)
    send_flat = send_slots.reshape(batch_size, local_veh, KMAX, channels, height * TILE)
    gathered, onehots = (
        lax.all_gather(send_flat, "veh", axis=1, tiled=True),
        lax.all_gather(own_onehot, "veh", axis=1, tiled=True),
    )
    gathered = gathered.reshape(batch_size, vehicles, KMAX, channels, height, TILE)
    partners = jnp.einsum(
        "bskt,bskchw->bschtw", onehots, gathered, preferred_element_type=jnp.float32
    ).astype(jnp.bfloat16)
    partners = partners.reshape(batch_size, vehicles, channels, height, breadth)
    col_mask = jnp.repeat(jnp.sum(onehots.astype(jnp.float32), axis=2), TILE, axis=-1)
    grad_full = (
        lax.all_gather(cotangent, "veh", axis=2, tiled=True).astype(jnp.float32) * ego_device
    )
    joined_map, self_weight, part_weight = join_agents(query, partners, col_mask, ego_embed)
    joined_bf = joined_map.astype(jnp.bfloat16)
    post_stack = tap_stack(pad_rows(joined_bf), height)
    post_pre = conv_apply(post_weight, post_stack)
    refined_full = joined_bf.astype(jnp.float32) + jax.nn.silu(post_pre)
    refined_full = refined_full.astype(jnp.bfloat16).astype(jnp.float32) * ego_device
    refined_bf = refined_full.astype(jnp.bfloat16)
    half_rows = height // devices_veh
    top_rows = refined_bf[:, :, :half_rows]
    bottom_rows = refined_bf[:, :, half_rows:]
    rows_low = lax.axis_index("veh") == 0
    rows_out = jnp.where(rows_low, bottom_rows, top_rows)
    rows_kept = jnp.where(rows_low, top_rows, bottom_rows)
    rows_in = lax.ppermute(rows_out, "veh", [(0, 1), (1, 0)])
    refined = (rows_kept.astype(jnp.float32) + rows_in.astype(jnp.float32)).astype(jnp.bfloat16)
    post_slope = (grad_full * silu_slope(post_pre)).astype(jnp.bfloat16)
    post_partial = weight_partial(post_stack, post_slope)
    weight_size = post_partial.size
    joined_grad = grad_full + conv_back(post_weight, tap_stack(pad_rows(post_slope), height))
    ego_term, part_grads, embed_partial = attend_back(
        query, partners, ego_embed, self_weight, part_weight, joined_grad
    )
    post_flat = jnp.concatenate([post_partial.reshape(-1), embed_partial])
    post_sum = lax.psum(post_flat, ("scene", "veh"))
    post_grad = post_sum[:weight_size].reshape(post_partial.shape)
    embed_grad = post_sum[weight_size:]
    part_tiles = part_grads.reshape(batch_size, vehicles, channels, height, tile_count, TILE)
    slot_grads = jnp.einsum(
        "bskt,bschtw->bskchw", onehots, part_tiles, preferred_element_type=jnp.float32
    )
    slot_grads = (
        slot_grads.reshape(batch_size, vehicles, KMAX, channels, height * TILE)
        * ego_device[:, :, :, :, None]
    )
    slot_bf = slot_grads.astype(jnp.bfloat16)
    low_half = slot_bf[:, :local_veh]
    high_half = slot_bf[:, local_veh:]
    on_low = lax.axis_index("veh") == 0
    outgoing = jnp.where(on_low, high_half, low_half)
    kept = jnp.where(on_low, low_half, high_half)
    incoming = lax.ppermute(outgoing, "veh", [(0, 1), (1, 0)])
    returned = (kept.astype(jnp.float32) + incoming.astype(jnp.float32)).astype(jnp.bfloat16)
    returned = returned.reshape(batch_size, local_veh, KMAX, channels, height, TILE)
    own_term = ego_mask[:, :, None, None, None] * ego_term.astype(jnp.float32)[:, None]
    placed = jnp.einsum(
        "bvkt,bvkchw->bvchtw", own_onehot, returned, preferred_element_type=jnp.float32
    )
    encoded_grad = own_term + placed.reshape(batch_size, local_veh, channels, height, breadth)
    encoded_grad = encoded_grad.reshape(batch_size * local_veh, channels, height, breadth)
    enc_slope = (encoded_grad * silu_slope(enc_pre)).astype(jnp.bfloat16)
    enc_partial = weight_partial(enc_stack, enc_slope)
    feature_grad = encoded_grad + conv_back(enc_weight, tap_stack(pad_rows(enc_slope), height))
    enc_grad = torus_psum(enc_partial.reshape(-1), parts=1).reshape(enc_partial.shape)
    return (
        refined,
        feature_grad.reshape(batch_size, local_veh, channels, height, breadth),
        enc_grad,
        post_grad,
        embed_grad,
    )


def solution(mesh):
    in_specs = (
        P("scene", "veh", None, None, None),
        P("scene"),
        P("scene"),
        P("scene", "veh", None),
        P("scene", "veh"),
        P(),
        P(),
        P(),
        P("scene", None, "veh", None),
    )
    out_specs = (P("scene", None, "veh", None), P("scene", "veh", None, None, None), P(), P(), P())
    return jax.shard_map(body, mesh=mesh, in_specs=in_specs, out_specs=out_specs, check_vma=False)
```

```python
import jax
import jax.numpy as jnp
from jax import lax
from jax.sharding import PartitionSpec as P

TILE = 32
KMAX = 2
LANES = 128


def ring_shift(stride, size, shift, total):
    pairs = []
    for source in range(total):
        place = (source // stride) % size
        pairs.append((source, source + (((place + shift) % size) - place) * stride))
    return pairs


def torus_psum(flat, parts=3):
    total = lax.axis_size("scene")
    side = round(total ** (1.0 / 3.0))
    axes = [(side * side, side), (side, side), (1, side)]
    veh_count = lax.axis_size("veh")
    length = flat.shape[0]
    unit = parts * veh_count * total * LANES
    padded = jnp.pad(flat, (0, (-length) % unit)).reshape(parts, -1, LANES)
    veh_id = lax.axis_index("veh")
    scene_id = lax.axis_index("scene")
    swap = [(0, 1), (1, 0)]
    results = []
    for part in range(parts):
        halves = padded[part].reshape(veh_count, -1, LANES)
        on_low = veh_id == 0
        outgoing = jnp.where(on_low, halves[1], halves[0])
        current = jnp.where(on_low, halves[0], halves[1]) + lax.ppermute(outgoing, "veh", swap)
        order = [axes[(part + k) % 3] for k in range(3)]
        for stride, size in order:
            place = (scene_id // stride) % size
            chunks = current.reshape(size, -1, LANES)
            current = lax.dynamic_index_in_dim(chunks, place, 0, keepdims=False)
            for shift in range(1, size):
                piece = lax.dynamic_index_in_dim(chunks, (place + shift) % size, 0, keepdims=False)
                current = current + lax.ppermute(piece, "scene", ring_shift(stride, size, shift, total))
        for stride, size in reversed(order):
            place = (scene_id // stride) % size
            got = [current] + [
                lax.ppermute(current, "scene", ring_shift(stride, size, shift, total))
                for shift in range(1, size)
            ]
            backward = jnp.concatenate(got[::-1] + got[::-1], axis=0)
            start = ((size - (place + 1) % size) % size) * current.shape[0]
            current = lax.dynamic_slice_in_dim(backward, start, size * current.shape[0], 0)
        other = lax.ppermute(current, "veh", swap)
        results.append(jnp.where(veh_id == 0, jnp.concatenate([current, other]), jnp.concatenate([other, current])))
    return jnp.stack(results).reshape(-1)[:length]


def pad_rows(source):
    return jnp.pad(source, [(0, 0)] * (source.ndim - 2) + [(2, 2), (0, 0)])


def tap_stack(padded, out_rows):
    breadth = padded.shape[-1]
    widened = jnp.pad(padded, [(0, 0)] * (padded.ndim - 1) + [(2, 2)])
    pieces = []
    for row_tap in range(3):
        for col_tap in range(3):
            pieces.append(
                widened[
                    ..., 2 * row_tap : 2 * row_tap + out_rows, 2 * col_tap : 2 * col_tap + breadth
                ]
            )
    return jnp.stack(pieces, axis=-4)


def conv_apply(weight, stacked):
    return jnp.einsum("tio,btirw->borw", weight, stacked, preferred_element_type=jnp.float32)


def conv_back(weight, stacked):
    return jnp.einsum("tio,btorw->birw", weight[::-1], stacked, preferred_element_type=jnp.float32)


def weight_partial(stacked, slope):
    return jnp.einsum("btirw,borw->tio", stacked, slope, preferred_element_type=jnp.float32)


def silu_slope(values):
    sigma = jax.nn.sigmoid(values)
    return sigma * (1.0 + values * (1.0 - sigma))


def join_agents(query, partners, col_mask, ego_embed):
    query_wide = query.astype(jnp.float32)
    parts_wide = partners.astype(jnp.float32)
    channel_count = query.shape[-3]
    key_self = query_wide + ego_embed.astype(jnp.float32)[:, None, None]
    score_self = jnp.sum(query_wide * key_self, axis=-3) / channel_count
    score_part = jnp.sum(query_wide[..., None, :, :, :] * parts_wide, axis=-3) / channel_count
    live_cells = col_mask[..., :, None, :] > 0.5
    row_max = jnp.maximum(score_self, jnp.max(jnp.where(live_cells, score_part, -jnp.inf), axis=-3))
    self_exp = jnp.exp(score_self - row_max)
    part_exp = jnp.where(
        live_cells, jnp.exp(jnp.minimum(score_part - row_max[..., None, :, :], 0.0)), 0.0
    )
    denominator = self_exp + jnp.sum(part_exp, axis=-3)
    self_weight = self_exp / denominator
    part_weight = part_exp / denominator[..., None, :, :]
    joined_map = self_weight[..., None, :, :] * query_wide + jnp.sum(
        part_weight[..., :, None, :, :] * parts_wide, axis=-4
    )
    return (joined_map, self_weight, part_weight)


def attend_back(query, partners, ego_embed, self_weight, part_weight, joined_grad):
    query_wide = query.astype(jnp.float32)
    parts_wide = partners.astype(jnp.float32)
    channel_count = query.shape[-3]
    self_dot = jnp.sum(joined_grad * query_wide, axis=-3)
    part_dot = jnp.sum(joined_grad[..., None, :, :, :] * parts_wide, axis=-3)
    mean_dot = self_weight * self_dot + jnp.sum(part_weight * part_dot, axis=-3)
    slope_self = self_weight * (self_dot - mean_dot)
    slope_part = part_weight * (part_dot - mean_dot[..., None, :, :])
    twice_key = 2.0 * query_wide + ego_embed.astype(jnp.float32)[:, None, None]
    ego_term = (
        self_weight[..., None, :, :] * joined_grad
        + (
            slope_self[..., None, :, :] * twice_key
            + jnp.sum(slope_part[..., :, None, :, :] * parts_wide, axis=-4)
        )
        / channel_count
    )
    part_grads = (
        part_weight[..., :, None, :, :] * joined_grad[..., None, :, :, :]
        + slope_part[..., :, None, :, :] * query_wide[..., None, :, :, :] / channel_count
    )
    embed_terms = jnp.sum(slope_self[..., None, :, :] * query_wide, axis=(-2, -1)) / channel_count
    embed_partial = jnp.sum(embed_terms, axis=0)
    return (ego_term.astype(jnp.bfloat16), part_grads.astype(jnp.bfloat16), embed_partial)


def body(
    features, counts, ego_ids, req_tiles, req_count, ego_embed, enc_weight, post_weight, cotangent
):
    batch_size, local_veh, channels, height, breadth = features.shape
    tile_count = breadth // TILE
    devices_veh = lax.axis_size("veh")
    vehicles = local_veh * devices_veh
    veh_here = lax.axis_index("veh") * local_veh + jnp.arange(local_veh)
    ego_local = ego_ids[:, None] == veh_here[None, :]
    ego_mask = ego_local.astype(jnp.float32)
    ego_device = jnp.sum(ego_mask, axis=1)[:, None, None, None]
    present = (veh_here[None, :] < counts[:, None]) & jnp.logical_not(ego_local)
    live_count = jnp.where(present, req_count, 0)
    slot_ids = jnp.arange(KMAX)
    tile_ids = jnp.arange(tile_count)
    own_onehot = (
        (req_tiles[:, :, :, None] == tile_ids[None, None, None, :])
        & (slot_ids[None, None, :, None] < live_count[:, :, None, None])
    ).astype(jnp.bfloat16)
    flat_maps = features.reshape(batch_size * local_veh, channels, height, breadth)
    enc_stack = tap_stack(pad_rows(flat_maps), height)
    enc_pre = conv_apply(enc_weight, enc_stack)
    encoded_flat = (flat_maps.astype(jnp.float32) + jax.nn.silu(enc_pre)).astype(jnp.bfloat16)
    encoded = encoded_flat.reshape(batch_size, local_veh, channels, height, breadth)
    query = jnp.einsum(
        "bv,bvchw->bchw", ego_mask.astype(jnp.bfloat16), encoded, preferred_element_type=jnp.float32
    ).astype(jnp.bfloat16)
    tiled_map = encoded.reshape(batch_size, local_veh, channels, height, tile_count, TILE)
    send_slots = jnp.einsum(
        "bvkt,bvchtw->bvkchw", own_onehot, tiled_map, preferred_element_type=jnp.float32
    ).astype(jnp.bfloat16)
    send_flat = send_slots.reshape(batch_size, local_veh, KMAX, channels, height * TILE)
    gathered, onehots = (
        lax.all_gather(send_flat, "veh", axis=1, tiled=True),
        lax.all_gather(own_onehot, "veh", axis=1, tiled=True),
    )
    gathered = gathered.reshape(batch_size, vehicles, KMAX, channels, height, TILE)
    partners = jnp.einsum(
        "bskt,bskchw->bschtw", onehots, gathered, preferred_element_type=jnp.float32
    ).astype(jnp.bfloat16)
    partners = partners.reshape(batch_size, vehicles, channels, height, breadth)
    col_mask = jnp.repeat(jnp.sum(onehots.astype(jnp.float32), axis=2), TILE, axis=-1)
    grad_full = (
        lax.all_gather(cotangent, "veh", axis=2, tiled=True).astype(jnp.float32) * ego_device
    )
    joined_map, self_weight, part_weight = join_agents(query, partners, col_mask, ego_embed)
    joined_bf = joined_map.astype(jnp.bfloat16)
    post_stack = tap_stack(pad_rows(joined_bf), height)
    post_pre = conv_apply(post_weight, post_stack)
    refined_full = joined_bf.astype(jnp.float32) + jax.nn.silu(post_pre)
    refined_full = refined_full.astype(jnp.bfloat16).astype(jnp.float32) * ego_device
    refined_bf = refined_full.astype(jnp.bfloat16)
    half_rows = height // devices_veh
    top_rows = refined_bf[:, :, :half_rows]
    bottom_rows = refined_bf[:, :, half_rows:]
    rows_low = lax.axis_index("veh") == 0
    rows_out = jnp.where(rows_low, bottom_rows, top_rows)
    rows_kept = jnp.where(rows_low, top_rows, bottom_rows)
    rows_in = lax.ppermute(rows_out, "veh", [(0, 1), (1, 0)])
    refined = (rows_kept.astype(jnp.float32) + rows_in.astype(jnp.float32)).astype(jnp.bfloat16)
    post_slope = (grad_full * silu_slope(post_pre)).astype(jnp.bfloat16)
    post_partial = weight_partial(post_stack, post_slope)
    weight_size = post_partial.size
    post_partial, post_slope = lax.optimization_barrier((post_partial, post_slope))
    post_grad = lax.psum(post_partial, ("scene", "veh"))
    joined_grad = grad_full + conv_back(post_weight, tap_stack(pad_rows(post_slope), height))
    ego_term, part_grads, embed_partial = attend_back(
        query, partners, ego_embed, self_weight, part_weight, joined_grad
    )
    part_tiles = part_grads.reshape(batch_size, vehicles, channels, height, tile_count, TILE)
    slot_grads = jnp.einsum(
        "bskt,bschtw->bskchw", onehots, part_tiles, preferred_element_type=jnp.float32
    )
    slot_grads = (
        slot_grads.reshape(batch_size, vehicles, KMAX, channels, height * TILE)
        * ego_device[:, :, :, :, None]
    )
    slot_bf = slot_grads.astype(jnp.bfloat16)
    low_half = slot_bf[:, :local_veh]
    high_half = slot_bf[:, local_veh:]
    on_low = lax.axis_index("veh") == 0
    outgoing = jnp.where(on_low, high_half, low_half)
    kept = jnp.where(on_low, low_half, high_half)
    incoming = lax.ppermute(outgoing, "veh", [(0, 1), (1, 0)])
    returned = (kept.astype(jnp.float32) + incoming.astype(jnp.float32)).astype(jnp.bfloat16)
    returned = returned.reshape(batch_size, local_veh, KMAX, channels, height, TILE)
    own_term = ego_mask[:, :, None, None, None] * ego_term.astype(jnp.float32)[:, None]
    placed = jnp.einsum(
        "bvkt,bvkchw->bvchtw", own_onehot, returned, preferred_element_type=jnp.float32
    )
    encoded_grad = own_term + placed.reshape(batch_size, local_veh, channels, height, breadth)
    encoded_grad = encoded_grad.reshape(batch_size * local_veh, channels, height, breadth)
    enc_slope = (encoded_grad * silu_slope(enc_pre)).astype(jnp.bfloat16)
    enc_partial = weight_partial(enc_stack, enc_slope)
    feature_grad = encoded_grad + conv_back(enc_weight, tap_stack(pad_rows(enc_slope), height))
    enc_flat = jnp.concatenate([enc_partial.reshape(-1), embed_partial])
    enc_sum = torus_psum(enc_flat, parts=1)
    enc_grad = enc_sum[:weight_size].reshape(enc_partial.shape)
    embed_grad = enc_sum[weight_size:]
    return (
        refined,
        feature_grad.reshape(batch_size, local_veh, channels, height, breadth),
        enc_grad,
        post_grad,
        embed_grad,
    )


def solution(mesh):
    in_specs = (
        P("scene", "veh", None, None, None),
        P("scene"),
        P("scene"),
        P("scene", "veh", None),
        P("scene", "veh"),
        P(),
        P(),
        P(),
        P("scene", None, "veh", None),
    )
    out_specs = (P("scene", None, "veh", None), P("scene", "veh", None, None, None), P(), P(), P())
    return jax.shard_map(body, mesh=mesh, in_specs=in_specs, out_specs=out_specs, check_vma=False)
```

```python
import jax
import jax.numpy as jnp
from jax import lax
from jax.sharding import PartitionSpec as P

TILE = 32
KMAX = 2
LANES = 256


def ring_shift(stride, size, shift, total):
    pairs = []
    for source in range(total):
        place = (source // stride) % size
        pairs.append((source, source + (((place + shift) % size) - place) * stride))
    return pairs


def torus_psum(flat, parts=3):
    total = lax.axis_size("scene")
    side = round(total ** (1.0 / 3.0))
    axes = [(side * side, side), (side, side), (1, side)]
    veh_count = lax.axis_size("veh")
    length = flat.shape[0]
    unit = parts * veh_count * total * LANES
    padded = jnp.pad(flat, (0, (-length) % unit)).reshape(parts, -1, LANES)
    veh_id = lax.axis_index("veh")
    scene_id = lax.axis_index("scene")
    swap = [(0, 1), (1, 0)]
    results = []
    for part in range(parts):
        halves = padded[part].reshape(veh_count, -1, LANES)
        on_low = veh_id == 0
        outgoing = jnp.where(on_low, halves[1], halves[0])
        current = jnp.where(on_low, halves[0], halves[1]) + lax.ppermute(outgoing, "veh", swap)
        order = [axes[(part + k) % 3] for k in range(3)]
        for stride, size in order:
            place = (scene_id // stride) % size
            chunks = current.reshape(size, -1, LANES)
            current = lax.dynamic_index_in_dim(chunks, place, 0, keepdims=False)
            for shift in range(1, size):
                piece = lax.dynamic_index_in_dim(chunks, (place + shift) % size, 0, keepdims=False)
                current = current + lax.ppermute(piece, "scene", ring_shift(stride, size, shift, total))
        for stride, size in reversed(order):
            place = (scene_id // stride) % size
            got = [current] + [
                lax.ppermute(current, "scene", ring_shift(stride, size, shift, total))
                for shift in range(1, size)
            ]
            backward = jnp.concatenate(got[::-1] + got[::-1], axis=0)
            start = ((size - (place + 1) % size) % size) * current.shape[0]
            current = lax.dynamic_slice_in_dim(backward, start, size * current.shape[0], 0)
        other = lax.ppermute(current, "veh", swap)
        first = jnp.where(on_low, current, other)
        second = jnp.where(on_low, other, current)
        results.append(jnp.concatenate([first, second]))
    return jnp.stack(results).reshape(-1)[:length]


def pad_rows(source):
    return jnp.pad(source, [(0, 0)] * (source.ndim - 2) + [(2, 2), (0, 0)])


def tap_stack(padded, out_rows):
    breadth = padded.shape[-1]
    widened = jnp.pad(padded, [(0, 0)] * (padded.ndim - 1) + [(2, 2)])
    pieces = []
    for row_tap in range(3):
        for col_tap in range(3):
            pieces.append(
                widened[
                    ..., 2 * row_tap : 2 * row_tap + out_rows, 2 * col_tap : 2 * col_tap + breadth
                ]
            )
    return jnp.stack(pieces, axis=-4)


def conv_apply(weight, stacked):
    return jnp.einsum("tio,btirw->borw", weight, stacked, preferred_element_type=jnp.float32)


def conv_back(weight, stacked):
    return jnp.einsum("tio,btorw->birw", weight[::-1], stacked, preferred_element_type=jnp.float32)


def weight_partial(stacked, slope):
    return jnp.einsum("btirw,borw->tio", stacked, slope, preferred_element_type=jnp.float32)


def silu_slope(values):
    sigma = jax.nn.sigmoid(values)
    return sigma * (1.0 + values * (1.0 - sigma))


def join_agents(query, partners, col_mask, ego_embed):
    query_wide = query.astype(jnp.float32)
    parts_wide = partners.astype(jnp.float32)
    channel_count = query.shape[-3]
    key_self = query_wide + ego_embed.astype(jnp.float32)[:, None, None]
    score_self = jnp.sum(query_wide * key_self, axis=-3) / channel_count
    score_part = jnp.sum(query_wide[..., None, :, :, :] * parts_wide, axis=-3) / channel_count
    live_cells = col_mask[..., :, None, :] > 0.5
    row_max = jnp.maximum(score_self, jnp.max(jnp.where(live_cells, score_part, -jnp.inf), axis=-3))
    self_exp = jnp.exp(score_self - row_max)
    part_exp = jnp.where(
        live_cells, jnp.exp(jnp.minimum(score_part - row_max[..., None, :, :], 0.0)), 0.0
    )
    denominator = self_exp + jnp.sum(part_exp, axis=-3)
    self_weight = self_exp / denominator
    part_weight = part_exp / denominator[..., None, :, :]
    joined_map = self_weight[..., None, :, :] * query_wide + jnp.sum(
        part_weight[..., :, None, :, :] * parts_wide, axis=-4
    )
    return (joined_map, self_weight, part_weight)


def attend_back(query, partners, ego_embed, self_weight, part_weight, joined_grad):
    query_wide = query.astype(jnp.float32)
    parts_wide = partners.astype(jnp.float32)
    channel_count = query.shape[-3]
    self_dot = jnp.sum(joined_grad * query_wide, axis=-3)
    part_dot = jnp.sum(joined_grad[..., None, :, :, :] * parts_wide, axis=-3)
    mean_dot = self_weight * self_dot + jnp.sum(part_weight * part_dot, axis=-3)
    slope_self = self_weight * (self_dot - mean_dot)
    slope_part = part_weight * (part_dot - mean_dot[..., None, :, :])
    twice_key = 2.0 * query_wide + ego_embed.astype(jnp.float32)[:, None, None]
    ego_term = (
        self_weight[..., None, :, :] * joined_grad
        + (
            slope_self[..., None, :, :] * twice_key
            + jnp.sum(slope_part[..., :, None, :, :] * parts_wide, axis=-4)
        )
        / channel_count
    )
    part_grads = (
        part_weight[..., :, None, :, :] * joined_grad[..., None, :, :, :]
        + slope_part[..., :, None, :, :] * query_wide[..., None, :, :, :] / channel_count
    )
    embed_terms = jnp.sum(slope_self[..., None, :, :] * query_wide, axis=(-2, -1)) / channel_count
    embed_partial = jnp.sum(embed_terms, axis=0)
    return (ego_term.astype(jnp.bfloat16), part_grads.astype(jnp.bfloat16), embed_partial)


def body(
    features, counts, ego_ids, req_tiles, req_count, ego_embed, enc_weight, post_weight, cotangent
):
    batch_size, local_veh, channels, height, breadth = features.shape
    tile_count = breadth // TILE
    devices_veh = lax.axis_size("veh")
    vehicles = local_veh * devices_veh
    veh_here = lax.axis_index("veh") * local_veh + jnp.arange(local_veh)
    ego_local = ego_ids[:, None] == veh_here[None, :]
    ego_mask = ego_local.astype(jnp.float32)
    ego_device = jnp.sum(ego_mask, axis=1)[:, None, None, None]
    present = (veh_here[None, :] < counts[:, None]) & jnp.logical_not(ego_local)
    live_count = jnp.where(present, req_count, 0)
    slot_ids = jnp.arange(KMAX)
    tile_ids = jnp.arange(tile_count)
    own_onehot = (
        (req_tiles[:, :, :, None] == tile_ids[None, None, None, :])
        & (slot_ids[None, None, :, None] < live_count[:, :, None, None])
    ).astype(jnp.bfloat16)
    flat_maps = features.reshape(batch_size * local_veh, channels, height, breadth)
    enc_stack = tap_stack(pad_rows(flat_maps), height)
    enc_pre = conv_apply(enc_weight, enc_stack)
    encoded_flat = (flat_maps.astype(jnp.float32) + jax.nn.silu(enc_pre)).astype(jnp.bfloat16)
    encoded = encoded_flat.reshape(batch_size, local_veh, channels, height, breadth)
    query = jnp.einsum(
        "bv,bvchw->bchw", ego_mask.astype(jnp.bfloat16), encoded, preferred_element_type=jnp.float32
    ).astype(jnp.bfloat16)
    tiled_map = encoded.reshape(batch_size, local_veh, channels, height, tile_count, TILE)
    send_slots = jnp.einsum(
        "bvkt,bvchtw->bvkchw", own_onehot, tiled_map, preferred_element_type=jnp.float32
    ).astype(jnp.bfloat16)
    send_flat = send_slots.reshape(batch_size, local_veh, KMAX, channels, height * TILE)
    gathered, onehots = (
        lax.all_gather(send_flat, "veh", axis=1, tiled=True),
        lax.all_gather(own_onehot, "veh", axis=1, tiled=True),
    )
    gathered = gathered.reshape(batch_size, vehicles, KMAX, channels, height, TILE)
    partners = jnp.einsum(
        "bskt,bskchw->bschtw", onehots, gathered, preferred_element_type=jnp.float32
    ).astype(jnp.bfloat16)
    partners = partners.reshape(batch_size, vehicles, channels, height, breadth)
    col_mask = jnp.repeat(jnp.sum(onehots.astype(jnp.float32), axis=2), TILE, axis=-1)
    grad_full = (
        lax.all_gather(cotangent, "veh", axis=2, tiled=True).astype(jnp.float32) * ego_device
    )
    joined_map, self_weight, part_weight = join_agents(query, partners, col_mask, ego_embed)
    joined_bf = joined_map.astype(jnp.bfloat16)
    post_stack = tap_stack(pad_rows(joined_bf), height)
    post_pre = conv_apply(post_weight, post_stack)
    refined_full = joined_bf.astype(jnp.float32) + jax.nn.silu(post_pre)
    refined_full = refined_full.astype(jnp.bfloat16).astype(jnp.float32) * ego_device
    refined_bf = refined_full.astype(jnp.bfloat16)
    half_rows = height // devices_veh
    top_rows = refined_bf[:, :, :half_rows]
    bottom_rows = refined_bf[:, :, half_rows:]
    rows_low = lax.axis_index("veh") == 0
    rows_out = jnp.where(rows_low, bottom_rows, top_rows)
    rows_kept = jnp.where(rows_low, top_rows, bottom_rows)
    rows_in = lax.ppermute(rows_out, "veh", [(0, 1), (1, 0)])
    refined = (rows_kept.astype(jnp.float32) + rows_in.astype(jnp.float32)).astype(jnp.bfloat16)
    post_slope = (grad_full * silu_slope(post_pre)).astype(jnp.bfloat16)
    post_partial = weight_partial(post_stack, post_slope)
    weight_size = post_partial.size
    post_partial, post_slope = lax.optimization_barrier((post_partial, post_slope))
    post_grad = lax.psum(post_partial, ("scene", "veh"))
    joined_grad = grad_full + conv_back(post_weight, tap_stack(pad_rows(post_slope), height))
    ego_term, part_grads, embed_partial = attend_back(
        query, partners, ego_embed, self_weight, part_weight, joined_grad
    )
    part_tiles = part_grads.reshape(batch_size, vehicles, channels, height, tile_count, TILE)
    slot_grads = jnp.einsum(
        "bskt,bschtw->bskchw", onehots, part_tiles, preferred_element_type=jnp.float32
    )
    slot_grads = (
        slot_grads.reshape(batch_size, vehicles, KMAX, channels, height * TILE)
        * ego_device[:, :, :, :, None]
    )
    slot_bf = slot_grads.astype(jnp.bfloat16)
    low_half = slot_bf[:, :local_veh]
    high_half = slot_bf[:, local_veh:]
    on_low = lax.axis_index("veh") == 0
    outgoing = jnp.where(on_low, high_half, low_half)
    kept = jnp.where(on_low, low_half, high_half)
    incoming = lax.ppermute(outgoing, "veh", [(0, 1), (1, 0)])
    returned = (kept.astype(jnp.float32) + incoming.astype(jnp.float32)).astype(jnp.bfloat16)
    returned = returned.reshape(batch_size, local_veh, KMAX, channels, height, TILE)
    own_term = ego_mask[:, :, None, None, None] * ego_term.astype(jnp.float32)[:, None]
    placed = jnp.einsum(
        "bvkt,bvkchw->bvchtw", own_onehot, returned, preferred_element_type=jnp.float32
    )
    encoded_grad = own_term + placed.reshape(batch_size, local_veh, channels, height, breadth)
    encoded_grad = encoded_grad.reshape(batch_size * local_veh, channels, height, breadth)
    enc_slope = (encoded_grad * silu_slope(enc_pre)).astype(jnp.bfloat16)
    enc_partial = weight_partial(enc_stack, enc_slope)
    feature_grad = encoded_grad + conv_back(enc_weight, tap_stack(pad_rows(enc_slope), height))
    enc_flat = jnp.concatenate([enc_partial.reshape(-1), embed_partial])
    enc_sum = torus_psum(enc_flat, parts=1)
    enc_grad = enc_sum[:weight_size].reshape(enc_partial.shape)
    embed_grad = enc_sum[weight_size:]
    return (
        refined,
        feature_grad.reshape(batch_size, local_veh, channels, height, breadth),
        enc_grad,
        post_grad,
        embed_grad,
    )


def solution(mesh):
    in_specs = (
        P("scene", "veh", None, None, None),
        P("scene"),
        P("scene"),
        P("scene", "veh", None),
        P("scene", "veh"),
        P(),
        P(),
        P(),
        P("scene", None, "veh", None),
    )
    out_specs = (P("scene", None, "veh", None), P("scene", "veh", None, None, None), P(), P(), P())
    return jax.shard_map(body, mesh=mesh, in_specs=in_specs, out_specs=out_specs, check_vma=False)
```

```python
import jax
import jax.numpy as jnp
from jax import lax
from jax.sharding import PartitionSpec as P

TILE = 32
KMAX = 2
LANES = 128


def ring_shift(stride, size, shift, total):
    pairs = []
    for source in range(total):
        place = (source // stride) % size
        pairs.append((source, source + (((place + shift) % size) - place) * stride))
    return pairs


def torus_psum(flat, parts=3, tied=None):
    total = lax.axis_size("scene")
    side = round(total ** (1.0 / 3.0))
    axes = [(side * side, side), (side, side), (1, side)]
    veh_count = lax.axis_size("veh")
    length = flat.shape[0]
    unit = parts * veh_count * total * LANES
    padded = jnp.pad(flat, (0, (-length) % unit)).reshape(parts, -1, LANES)
    veh_id = lax.axis_index("veh")
    scene_id = lax.axis_index("scene")
    swap = [(0, 1), (1, 0)]
    results = []
    for part in range(parts):
        halves = padded[part].reshape(veh_count, -1, LANES)
        on_low = veh_id == 0
        outgoing = jnp.where(on_low, halves[1], halves[0])
        current = jnp.where(on_low, halves[0], halves[1]) + lax.ppermute(outgoing, "veh", swap)
        order = [axes[(part + k) % 3] for k in range(3)]
        for stride, size in order:
            place = (scene_id // stride) % size
            chunks = current.reshape(size, -1, LANES)
            current = lax.dynamic_index_in_dim(chunks, place, 0, keepdims=False)
            for shift in range(1, size):
                piece = lax.dynamic_index_in_dim(chunks, (place + shift) % size, 0, keepdims=False)
                current = current + lax.ppermute(piece, "scene", ring_shift(stride, size, shift, total))
            if tied is not None:
                current, tied = lax.optimization_barrier((current, tied))
        for stride, size in reversed(order):
            place = (scene_id // stride) % size
            got = [current] + [
                lax.ppermute(current, "scene", ring_shift(stride, size, shift, total))
                for shift in range(1, size)
            ]
            backward = jnp.concatenate(got[::-1] + got[::-1], axis=0)
            start = ((size - (place + 1) % size) % size) * current.shape[0]
            current = lax.dynamic_slice_in_dim(backward, start, size * current.shape[0], 0)
        other = lax.ppermute(current, "veh", swap)
        results.append(jnp.where(veh_id == 0, jnp.concatenate([current, other]), jnp.concatenate([other, current])))
    return jnp.stack(results).reshape(-1)[:length], tied


def pad_rows(source):
    return jnp.pad(source, [(0, 0)] * (source.ndim - 2) + [(2, 2), (0, 0)])


def tap_stack(padded, out_rows):
    breadth = padded.shape[-1]
    widened = jnp.pad(padded, [(0, 0)] * (padded.ndim - 1) + [(2, 2)])
    pieces = []
    for row_tap in range(3):
        for col_tap in range(3):
            pieces.append(
                widened[
                    ..., 2 * row_tap : 2 * row_tap + out_rows, 2 * col_tap : 2 * col_tap + breadth
                ]
            )
    return jnp.stack(pieces, axis=-4)


def conv_apply(weight, stacked):
    return jnp.einsum("tio,btirw->borw", weight, stacked, preferred_element_type=jnp.float32)


def conv_back(weight, stacked):
    return jnp.einsum("tio,btorw->birw", weight[::-1], stacked, preferred_element_type=jnp.float32)


def weight_partial(stacked, slope):
    return jnp.einsum("btirw,borw->tio", stacked, slope, preferred_element_type=jnp.float32)


def silu_slope(values):
    sigma = jax.nn.sigmoid(values)
    return sigma * (1.0 + values * (1.0 - sigma))


def join_agents(query, partners, col_mask, ego_embed):
    query_wide = query.astype(jnp.float32)
    parts_wide = partners.astype(jnp.float32)
    channel_count = query.shape[-3]
    key_self = query_wide + ego_embed.astype(jnp.float32)[:, None, None]
    score_self = jnp.sum(query_wide * key_self, axis=-3) / channel_count
    score_part = jnp.sum(query_wide[..., None, :, :, :] * parts_wide, axis=-3) / channel_count
    live_cells = col_mask[..., :, None, :] > 0.5
    row_max = jnp.maximum(score_self, jnp.max(jnp.where(live_cells, score_part, -jnp.inf), axis=-3))
    self_exp = jnp.exp(score_self - row_max)
    part_exp = jnp.where(
        live_cells, jnp.exp(jnp.minimum(score_part - row_max[..., None, :, :], 0.0)), 0.0
    )
    denominator = self_exp + jnp.sum(part_exp, axis=-3)
    self_weight = self_exp / denominator
    part_weight = part_exp / denominator[..., None, :, :]
    joined_map = self_weight[..., None, :, :] * query_wide + jnp.sum(
        part_weight[..., :, None, :, :] * parts_wide, axis=-4
    )
    return (joined_map, self_weight, part_weight)


def attend_back(query, partners, ego_embed, self_weight, part_weight, joined_grad):
    query_wide = query.astype(jnp.float32)
    parts_wide = partners.astype(jnp.float32)
    channel_count = query.shape[-3]
    self_dot = jnp.sum(joined_grad * query_wide, axis=-3)
    part_dot = jnp.sum(joined_grad[..., None, :, :, :] * parts_wide, axis=-3)
    mean_dot = self_weight * self_dot + jnp.sum(part_weight * part_dot, axis=-3)
    slope_self = self_weight * (self_dot - mean_dot)
    slope_part = part_weight * (part_dot - mean_dot[..., None, :, :])
    twice_key = 2.0 * query_wide + ego_embed.astype(jnp.float32)[:, None, None]
    ego_term = (
        self_weight[..., None, :, :] * joined_grad
        + (
            slope_self[..., None, :, :] * twice_key
            + jnp.sum(slope_part[..., :, None, :, :] * parts_wide, axis=-4)
        )
        / channel_count
    )
    part_grads = (
        part_weight[..., :, None, :, :] * joined_grad[..., None, :, :, :]
        + slope_part[..., :, None, :, :] * query_wide[..., None, :, :, :] / channel_count
    )
    embed_terms = jnp.sum(slope_self[..., None, :, :] * query_wide, axis=(-2, -1)) / channel_count
    embed_partial = jnp.sum(embed_terms, axis=0)
    return (ego_term.astype(jnp.bfloat16), part_grads.astype(jnp.bfloat16), embed_partial)


def body(
    features, counts, ego_ids, req_tiles, req_count, ego_embed, enc_weight, post_weight, cotangent
):
    batch_size, local_veh, channels, height, breadth = features.shape
    tile_count = breadth // TILE
    devices_veh = lax.axis_size("veh")
    vehicles = local_veh * devices_veh
    veh_here = lax.axis_index("veh") * local_veh + jnp.arange(local_veh)
    ego_local = ego_ids[:, None] == veh_here[None, :]
    ego_mask = ego_local.astype(jnp.float32)
    ego_device = jnp.sum(ego_mask, axis=1)[:, None, None, None]
    present = (veh_here[None, :] < counts[:, None]) & jnp.logical_not(ego_local)
    live_count = jnp.where(present, req_count, 0)
    slot_ids = jnp.arange(KMAX)
    tile_ids = jnp.arange(tile_count)
    own_onehot = (
        (req_tiles[:, :, :, None] == tile_ids[None, None, None, :])
        & (slot_ids[None, None, :, None] < live_count[:, :, None, None])
    ).astype(jnp.bfloat16)
    flat_maps = features.reshape(batch_size * local_veh, channels, height, breadth)
    enc_stack = tap_stack(pad_rows(flat_maps), height)
    enc_pre = conv_apply(enc_weight, enc_stack)
    encoded_flat = (flat_maps.astype(jnp.float32) + jax.nn.silu(enc_pre)).astype(jnp.bfloat16)
    encoded = encoded_flat.reshape(batch_size, local_veh, channels, height, breadth)
    query = jnp.einsum(
        "bv,bvchw->bchw", ego_mask.astype(jnp.bfloat16), encoded, preferred_element_type=jnp.float32
    ).astype(jnp.bfloat16)
    tiled_map = encoded.reshape(batch_size, local_veh, channels, height, tile_count, TILE)
    send_slots = jnp.einsum(
        "bvkt,bvchtw->bvkchw", own_onehot, tiled_map, preferred_element_type=jnp.float32
    ).astype(jnp.bfloat16)
    send_flat = send_slots.reshape(batch_size, local_veh, KMAX, channels, height * TILE)
    gathered, onehots = (
        lax.all_gather(send_flat, "veh", axis=1, tiled=True),
        lax.all_gather(own_onehot, "veh", axis=1, tiled=True),
    )
    gathered = gathered.reshape(batch_size, vehicles, KMAX, channels, height, TILE)
    partners = jnp.einsum(
        "bskt,bskchw->bschtw", onehots, gathered, preferred_element_type=jnp.float32
    ).astype(jnp.bfloat16)
    partners = partners.reshape(batch_size, vehicles, channels, height, breadth)
    col_mask = jnp.repeat(jnp.sum(onehots.astype(jnp.float32), axis=2), TILE, axis=-1)
    grad_full = (
        lax.all_gather(cotangent, "veh", axis=2, tiled=True).astype(jnp.float32) * ego_device
    )
    joined_map, self_weight, part_weight = join_agents(query, partners, col_mask, ego_embed)
    joined_bf = joined_map.astype(jnp.bfloat16)
    post_stack = tap_stack(pad_rows(joined_bf), height)
    post_pre = conv_apply(post_weight, post_stack)
    refined_full = joined_bf.astype(jnp.float32) + jax.nn.silu(post_pre)
    refined_full = refined_full.astype(jnp.bfloat16).astype(jnp.float32) * ego_device
    refined_bf = refined_full.astype(jnp.bfloat16)
    half_rows = height // devices_veh
    top_rows = refined_bf[:, :, :half_rows]
    bottom_rows = refined_bf[:, :, half_rows:]
    rows_low = lax.axis_index("veh") == 0
    rows_out = jnp.where(rows_low, bottom_rows, top_rows)
    rows_kept = jnp.where(rows_low, top_rows, bottom_rows)
    rows_in = lax.ppermute(rows_out, "veh", [(0, 1), (1, 0)])
    refined = (rows_kept.astype(jnp.float32) + rows_in.astype(jnp.float32)).astype(jnp.bfloat16)
    post_slope = (grad_full * silu_slope(post_pre)).astype(jnp.bfloat16)
    post_partial = weight_partial(post_stack, post_slope)
    weight_size = post_partial.size
    post_partial, post_slope = lax.optimization_barrier((post_partial, post_slope))
    post_grad = lax.psum(post_partial, ("scene", "veh"))
    joined_grad = grad_full + conv_back(post_weight, tap_stack(pad_rows(post_slope), height))
    ego_term, part_grads, embed_partial = attend_back(
        query, partners, ego_embed, self_weight, part_weight, joined_grad
    )
    part_tiles = part_grads.reshape(batch_size, vehicles, channels, height, tile_count, TILE)
    slot_grads = jnp.einsum(
        "bskt,bschtw->bskchw", onehots, part_tiles, preferred_element_type=jnp.float32
    )
    slot_grads = (
        slot_grads.reshape(batch_size, vehicles, KMAX, channels, height * TILE)
        * ego_device[:, :, :, :, None]
    )
    slot_bf = slot_grads.astype(jnp.bfloat16)
    low_half = slot_bf[:, :local_veh]
    high_half = slot_bf[:, local_veh:]
    on_low = lax.axis_index("veh") == 0
    outgoing = jnp.where(on_low, high_half, low_half)
    kept = jnp.where(on_low, low_half, high_half)
    incoming = lax.ppermute(outgoing, "veh", [(0, 1), (1, 0)])
    returned = (kept.astype(jnp.float32) + incoming.astype(jnp.float32)).astype(jnp.bfloat16)
    returned = returned.reshape(batch_size, local_veh, KMAX, channels, height, TILE)
    own_term = ego_mask[:, :, None, None, None] * ego_term.astype(jnp.float32)[:, None]
    placed = jnp.einsum(
        "bvkt,bvkchw->bvchtw", own_onehot, returned, preferred_element_type=jnp.float32
    )
    encoded_grad = own_term + placed.reshape(batch_size, local_veh, channels, height, breadth)
    encoded_grad = encoded_grad.reshape(batch_size * local_veh, channels, height, breadth)
    enc_slope = (encoded_grad * silu_slope(enc_pre)).astype(jnp.bfloat16)
    enc_partial = weight_partial(enc_stack, enc_slope)
    feature_grad = encoded_grad + conv_back(enc_weight, tap_stack(pad_rows(enc_slope), height))
    enc_flat = jnp.concatenate([enc_partial.reshape(-1), embed_partial])
    enc_sum, feature_grad = torus_psum(enc_flat, parts=1, tied=feature_grad)
    enc_grad = enc_sum[:weight_size].reshape(enc_partial.shape)
    embed_grad = enc_sum[weight_size:]
    return (
        refined,
        feature_grad.reshape(batch_size, local_veh, channels, height, breadth),
        enc_grad,
        post_grad,
        embed_grad,
    )


def solution(mesh):
    in_specs = (
        P("scene", "veh", None, None, None),
        P("scene"),
        P("scene"),
        P("scene", "veh", None),
        P("scene", "veh"),
        P(),
        P(),
        P(),
        P("scene", None, "veh", None),
    )
    out_specs = (P("scene", None, "veh", None), P("scene", "veh", None, None, None), P(), P(), P())
    return jax.shard_map(body, mesh=mesh, in_specs=in_specs, out_specs=out_specs, check_vma=False)
```

```python
import jax
import jax.numpy as jnp
from jax import lax
from jax.sharding import PartitionSpec as P

TILE = 32
KMAX = 2
LANES = 128


def ring_shift(stride, size, shift, total):
    pairs = []
    for source in range(total):
        place = (source // stride) % size
        pairs.append((source, source + (((place + shift) % size) - place) * stride))
    return pairs


def torus_psum(flat, parts=3):
    total = lax.axis_size("scene")
    side = round(total ** (1.0 / 3.0))
    axes = [(side * side, side), (side, side), (1, side)]
    veh_count = lax.axis_size("veh")
    length = flat.shape[0]
    unit = parts * veh_count * total * LANES
    padded = jnp.pad(flat, (0, (-length) % unit)).reshape(parts, -1, LANES)
    veh_id = lax.axis_index("veh")
    scene_id = lax.axis_index("scene")
    swap = [(0, 1), (1, 0)]
    results = []
    for part in range(parts):
        halves = padded[part].reshape(veh_count, -1, LANES)
        on_low = veh_id == 0
        outgoing = jnp.where(on_low, halves[1], halves[0])
        current = jnp.where(on_low, halves[0], halves[1]) + lax.ppermute(outgoing, "veh", swap)
        order = [axes[(part + k) % 3] for k in range(3)]
        for stride, size in order:
            place = (scene_id // stride) % size
            chunks = current.reshape(size, -1, LANES)
            current = lax.dynamic_index_in_dim(chunks, place, 0, keepdims=False)
            for shift in range(1, size):
                piece = lax.dynamic_index_in_dim(chunks, (place + shift) % size, 0, keepdims=False)
                current = current + lax.ppermute(piece, "scene", ring_shift(stride, size, shift, total))
        for stride, size in reversed(order):
            place = (scene_id // stride) % size
            got = [current] + [
                lax.ppermute(current, "scene", ring_shift(stride, size, shift, total))
                for shift in range(1, size)
            ]
            backward = jnp.concatenate(got[::-1] + got[::-1], axis=0)
            start = ((size - (place + 1) % size) % size) * current.shape[0]
            current = lax.dynamic_slice_in_dim(backward, start, size * current.shape[0], 0)
        other = lax.ppermute(current, "veh", swap)
        first = jnp.where(on_low, current, other)
        second = jnp.where(on_low, other, current)
        results.append(jnp.concatenate([first, second]))
    return jnp.stack(results).reshape(-1)[:length]


def pad_rows(source):
    return jnp.pad(source, [(0, 0)] * (source.ndim - 2) + [(2, 2), (0, 0)])


def tap_stack(padded, out_rows):
    breadth = padded.shape[-1]
    widened = jnp.pad(padded, [(0, 0)] * (padded.ndim - 1) + [(2, 2)])
    pieces = []
    for row_tap in range(3):
        for col_tap in range(3):
            pieces.append(
                widened[
                    ..., 2 * row_tap : 2 * row_tap + out_rows, 2 * col_tap : 2 * col_tap + breadth
                ]
            )
    return jnp.stack(pieces, axis=-4)


def conv_apply(weight, stacked):
    return jnp.einsum("tio,btirw->borw", weight, stacked, preferred_element_type=jnp.float32)


def conv_back(weight, stacked):
    return jnp.einsum("tio,btorw->birw", weight[::-1], stacked, preferred_element_type=jnp.float32)


def weight_partial(stacked, slope):
    return jnp.einsum("btirw,borw->tio", stacked, slope, preferred_element_type=jnp.float32)


def silu_slope(values):
    sigma = jax.nn.sigmoid(values)
    return sigma * (1.0 + values * (1.0 - sigma))


def join_agents(query, partners, col_mask, ego_embed):
    query_wide = query.astype(jnp.float32)
    parts_wide = partners.astype(jnp.float32)
    channel_count = query.shape[-3]
    key_self = query_wide + ego_embed.astype(jnp.float32)[:, None, None]
    score_self = jnp.sum(query_wide * key_self, axis=-3) / channel_count
    score_part = jnp.sum(query_wide[..., None, :, :, :] * parts_wide, axis=-3) / channel_count
    live_cells = col_mask[..., :, None, :] > 0.5
    row_max = jnp.maximum(score_self, jnp.max(jnp.where(live_cells, score_part, -jnp.inf), axis=-3))
    self_exp = jnp.exp(score_self - row_max)
    part_exp = jnp.where(
        live_cells, jnp.exp(jnp.minimum(score_part - row_max[..., None, :, :], 0.0)), 0.0
    )
    denominator = self_exp + jnp.sum(part_exp, axis=-3)
    self_weight = self_exp / denominator
    part_weight = part_exp / denominator[..., None, :, :]
    joined_map = self_weight[..., None, :, :] * query_wide + jnp.sum(
        part_weight[..., :, None, :, :] * parts_wide, axis=-4
    )
    return (joined_map, self_weight, part_weight)


def attend_back(query, partners, ego_embed, self_weight, part_weight, joined_grad):
    query_wide = query.astype(jnp.float32)
    parts_wide = partners.astype(jnp.float32)
    channel_count = query.shape[-3]
    self_dot = jnp.sum(joined_grad * query_wide, axis=-3)
    part_dot = jnp.sum(joined_grad[..., None, :, :, :] * parts_wide, axis=-3)
    mean_dot = self_weight * self_dot + jnp.sum(part_weight * part_dot, axis=-3)
    slope_self = self_weight * (self_dot - mean_dot)
    slope_part = part_weight * (part_dot - mean_dot[..., None, :, :])
    twice_key = 2.0 * query_wide + ego_embed.astype(jnp.float32)[:, None, None]
    ego_term = (
        self_weight[..., None, :, :] * joined_grad
        + (
            slope_self[..., None, :, :] * twice_key
            + jnp.sum(slope_part[..., :, None, :, :] * parts_wide, axis=-4)
        )
        / channel_count
    )
    part_grads = (
        part_weight[..., :, None, :, :] * joined_grad[..., None, :, :, :]
        + slope_part[..., :, None, :, :] * query_wide[..., None, :, :, :] / channel_count
    )
    embed_terms = jnp.sum(slope_self[..., None, :, :] * query_wide, axis=(-2, -1)) / channel_count
    embed_partial = jnp.sum(embed_terms, axis=0)
    return (ego_term.astype(jnp.bfloat16), part_grads.astype(jnp.bfloat16), embed_partial)


def body(
    features, counts, ego_ids, req_tiles, req_count, ego_embed, enc_weight, post_weight, cotangent
):
    batch_size, local_veh, channels, height, breadth = features.shape
    tile_count = breadth // TILE
    devices_veh = lax.axis_size("veh")
    vehicles = local_veh * devices_veh
    veh_here = lax.axis_index("veh") * local_veh + jnp.arange(local_veh)
    ego_local = ego_ids[:, None] == veh_here[None, :]
    ego_mask = ego_local.astype(jnp.float32)
    ego_device = jnp.sum(ego_mask, axis=1)[:, None, None, None]
    present = (veh_here[None, :] < counts[:, None]) & jnp.logical_not(ego_local)
    live_count = jnp.where(present, req_count, 0)
    slot_ids = jnp.arange(KMAX)
    tile_ids = jnp.arange(tile_count)
    own_onehot = (
        (req_tiles[:, :, :, None] == tile_ids[None, None, None, :])
        & (slot_ids[None, None, :, None] < live_count[:, :, None, None])
    ).astype(jnp.bfloat16)
    flat_maps = features.reshape(batch_size * local_veh, channels, height, breadth)
    enc_stack = tap_stack(pad_rows(flat_maps), height)
    enc_pre = conv_apply(enc_weight, enc_stack)
    encoded_flat = (flat_maps.astype(jnp.float32) + jax.nn.silu(enc_pre)).astype(jnp.bfloat16)
    encoded = encoded_flat.reshape(batch_size, local_veh, channels, height, breadth)
    query = jnp.einsum(
        "bv,bvchw->bchw", ego_mask.astype(jnp.bfloat16), encoded, preferred_element_type=jnp.float32
    ).astype(jnp.bfloat16)
    tiled_map = encoded.reshape(batch_size, local_veh, channels, height, tile_count, TILE)
    send_slots = jnp.einsum(
        "bvkt,bvchtw->bvkchw", own_onehot, tiled_map, preferred_element_type=jnp.float32
    ).astype(jnp.bfloat16)
    send_flat = send_slots.reshape(batch_size, local_veh, KMAX, channels, height * TILE)
    gathered, onehots = (
        lax.all_gather(send_flat, "veh", axis=1, tiled=True),
        lax.all_gather(own_onehot, "veh", axis=1, tiled=True),
    )
    gathered = gathered.reshape(batch_size, vehicles, KMAX, channels, height, TILE)
    partners = jnp.einsum(
        "bskt,bskchw->bschtw", onehots, gathered, preferred_element_type=jnp.float32
    ).astype(jnp.bfloat16)
    partners = partners.reshape(batch_size, vehicles, channels, height, breadth)
    col_mask = jnp.repeat(jnp.sum(onehots.astype(jnp.float32), axis=2), TILE, axis=-1)
    grad_full = (
        lax.all_gather(cotangent, "veh", axis=2, tiled=True).astype(jnp.float32) * ego_device
    )
    joined_map, self_weight, part_weight = join_agents(query, partners, col_mask, ego_embed)
    joined_bf = joined_map.astype(jnp.bfloat16)
    post_stack = tap_stack(pad_rows(joined_bf), height)
    post_pre = conv_apply(post_weight, post_stack)
    refined_full = joined_bf.astype(jnp.float32) + jax.nn.silu(post_pre)
    refined_full = refined_full.astype(jnp.bfloat16).astype(jnp.float32) * ego_device
    refined_bf = refined_full.astype(jnp.bfloat16)
    half_rows = height // devices_veh
    top_rows = refined_bf[:, :, :half_rows]
    bottom_rows = refined_bf[:, :, half_rows:]
    rows_low = lax.axis_index("veh") == 0
    rows_out = jnp.where(rows_low, bottom_rows, top_rows)
    rows_kept = jnp.where(rows_low, top_rows, bottom_rows)
    rows_in = lax.ppermute(rows_out, "veh", [(0, 1), (1, 0)])
    refined = (rows_kept.astype(jnp.float32) + rows_in.astype(jnp.float32)).astype(jnp.bfloat16)
    post_slope = (grad_full * silu_slope(post_pre)).astype(jnp.bfloat16)
    post_partial = weight_partial(post_stack, post_slope)
    weight_size = post_partial.size
    post_partial, post_slope = lax.optimization_barrier((post_partial, post_slope))
    post_grad = lax.psum(post_partial, ("scene", "veh"))
    joined_grad = grad_full + conv_back(post_weight, tap_stack(pad_rows(post_slope), height))
    ego_term, part_grads, embed_partial = attend_back(
        query, partners, ego_embed, self_weight, part_weight, joined_grad
    )
    part_tiles = part_grads.reshape(batch_size, vehicles, channels, height, tile_count, TILE)
    slot_grads = jnp.einsum(
        "bskt,bschtw->bskchw", onehots, part_tiles, preferred_element_type=jnp.float32
    )
    slot_grads = (
        slot_grads.reshape(batch_size, vehicles, KMAX, channels, height * TILE)
        * ego_device[:, :, :, :, None]
    )
    slot_bf = slot_grads.astype(jnp.bfloat16)
    low_half = slot_bf[:, :local_veh]
    high_half = slot_bf[:, local_veh:]
    on_low = lax.axis_index("veh") == 0
    outgoing = jnp.where(on_low, high_half, low_half)
    kept = jnp.where(on_low, low_half, high_half)
    incoming = lax.ppermute(outgoing, "veh", [(0, 1), (1, 0)])
    returned = (kept.astype(jnp.float32) + incoming.astype(jnp.float32)).astype(jnp.bfloat16)
    returned = returned.reshape(batch_size, local_veh, KMAX, channels, height, TILE)
    own_term = ego_mask[:, :, None, None, None] * ego_term.astype(jnp.float32)[:, None]
    placed = jnp.einsum(
        "bvkt,bvkchw->bvchtw", own_onehot, returned, preferred_element_type=jnp.float32
    )
    encoded_grad = own_term + placed.reshape(batch_size, local_veh, channels, height, breadth)
    encoded_grad = encoded_grad.reshape(batch_size * local_veh, channels, height, breadth)
    enc_slope = (encoded_grad * silu_slope(enc_pre)).astype(jnp.bfloat16)
    enc_partial = weight_partial(enc_stack, enc_slope)
    feature_grad = encoded_grad + conv_back(enc_weight, tap_stack(pad_rows(enc_slope), height))
    enc_flat = jnp.concatenate([enc_partial.reshape(-1), embed_partial])
    enc_sum = torus_psum(enc_flat, parts=1)
    enc_grad = enc_sum[:weight_size].reshape(enc_partial.shape)
    embed_grad = enc_sum[weight_size:]
    return (
        refined,
        feature_grad.reshape(batch_size, local_veh, channels, height, breadth),
        enc_grad,
        post_grad,
        embed_grad,
    )


def solution(mesh):
    in_specs = (
        P("scene", "veh", None, None, None),
        P("scene"),
        P("scene"),
        P("scene", "veh", None),
        P("scene", "veh"),
        P(),
        P(),
        P(),
        P("scene", None, "veh", None),
    )
    out_specs = (P("scene", None, "veh", None), P("scene", "veh", None, None, None), P(), P(), P())
    return jax.shard_map(body, mesh=mesh, in_specs=in_specs, out_specs=out_specs, check_vma=False)
```
